768 devices in a mesh: space: 24 (over x, z_hi, core), energy: 32 (over z_lo, y).
Axes of the slice: x: 4, y: 8, z: 12 (z_hi: 3, z_lo: 4; z = z_hi * 4 + z_lo), core: 2. Of those that a mesh axis runs over, the one named last changes fastest.
Arguments:
- green_lower: bfloat16 [24, 128, 2, 128, 128], P('space', 'energy'), may hold values from -0.5 to 0.5
- green_diag: bfloat16 [24, 128, 2, 128, 128], P('space', 'energy'), may hold values from -0.5 to 0.5
- green_upper: bfloat16 [24, 128, 2, 128, 128], P('space', 'energy'), may hold values from -0.5 to 0.5
- self_energy: bfloat16 [2, 24, 128, 2, 128, 128], P(None, 'space', 'energy'), may hold values from -1.75 to 1.75
- coulomb: bfloat16 [24, 128, 128], P('space'), may hold values from -0.5 to 0.5
Outputs:
- screened_polarization: bfloat16 [2, 24, 128, 2, 128, 128], P(None, 'space', 'energy')
The draws below stay inside these ranges and needn't reach their ends.
All inputs are finite; a program needn't handle non-finite values.
Results may differ from the reference program's by a relative error of at most 0.017.
Values may be sent and summed in bfloat16 or wider, within the bound.
No kernel may reach another device: no remote copies, remote signals or barrier semaphores. Data moves between devices by JAX's collectives and lax.ppermute only.
A program may use at most 64 MiB of HBM per device.

```python
import jax
import jax.numpy as jnp
from jax import lax

B = 128
NBLOCKS = 24
ENERGIES = 128
PADDED = 256


def shard_levels(stream_key, shape, shards, low, largest):
    factor_of = 1.0
    for dim, parts in shards:
        heights = jax.random.uniform(jax.random.fold_in(jax.random.fold_in(stream_key, 6), dim), (parts,), jnp.float32, low / len(shards), largest / len(shards))
        factor_of = factor_of * jnp.repeat(jnp.exp(heights), shape[dim] // parts).reshape((-1,) + (1,) * (len(shape) - 1 - dim))
    return factor_of


def noise(own_key, shape, width, bound, cuts=(), held_as=jnp.bfloat16):
    gain = shard_levels(own_key, shape, cuts, -0.22, 0.18) if cuts else 1.0
    values = jax.random.normal(own_key, shape, jnp.float32) * width * gain
    return jnp.minimum(jnp.maximum(values, -bound), bound).astype(held_as)


def setup_inputs(seed: int = 0) -> dict:
    arg_keys = jax.random.split(jax.random.key(seed), 6)
    green_lower = noise(arg_keys[0], (NBLOCKS, ENERGIES, 2, B, B), B ** -0.5, 0.5, ((0, 24), (1, 32)))
    green_diag = noise(arg_keys[1], (NBLOCKS, ENERGIES, 2, B, B), B ** -0.5, 0.5, ((0, 24), (1, 32)))
    green_upper = noise(arg_keys[2], (NBLOCKS, ENERGIES, 2, B, B), B ** -0.5, 0.5, ((0, 24), (1, 32)))
    self_energy = noise(arg_keys[3], (2, NBLOCKS, ENERGIES, 2, B, B), 0.3, 1.75, ((1, 24), (2, 32)))
    coulomb = noise(arg_keys[4], (NBLOCKS, B, B), B ** -0.5, 0.5, ((0, 24),))
    return {"green_lower": green_lower, "green_diag": green_diag, "green_upper": green_upper, "self_energy": self_energy, "coulomb": coulomb}


def to_bfloat(values):
    return lax.optimization_barrier(values.astype(jnp.bfloat16)).astype(jnp.float32)


def congruence(green, sigma):
    green = green.astype(jnp.float32)
    sigma = sigma.astype(jnp.float32)
    green_real = green[:, 0]
    green_imag = green[:, 1]
    sigma_real = sigma[:, :, 0]
    sigma_imag = sigma[:, :, 1]
    mixed_real = to_bfloat(jnp.einsum('epq,feqr->fepr', green_real, sigma_real) - jnp.einsum('epq,feqr->fepr', green_imag, sigma_imag))
    mixed_imag = to_bfloat(jnp.einsum('epq,feqr->fepr', green_real, sigma_imag) + jnp.einsum('epq,feqr->fepr', green_imag, sigma_real))
    result_real = jnp.einsum('fepr,esr->feps', mixed_real, green_real) + jnp.einsum('fepr,esr->feps', mixed_imag, green_imag)
    result_imag = jnp.einsum('fepr,esr->feps', mixed_imag, green_real) - jnp.einsum('fepr,esr->feps', mixed_real, green_imag)
    return result_real, result_imag


def reference(green_lower, green_diag, green_upper, self_energy, coulomb):
    sigma_padded = jnp.pad(self_energy, ((0, 0), (1, 1), (0, 0), (0, 0), (0, 0), (0, 0)))
    factor = ENERGIES ** -0.5

    def one_block(block_id):
        lower_green = lax.dynamic_index_in_dim(green_lower, block_id, 0, keepdims=False)
        diag_green = lax.dynamic_index_in_dim(green_diag, block_id, 0, keepdims=False)
        upper_green = lax.dynamic_index_in_dim(green_upper, block_id, 0, keepdims=False)
        window = lax.dynamic_slice_in_dim(sigma_padded, block_id, 3, 1)
        first = congruence(lower_green, window[:, 0])
        second = congruence(diag_green, window[:, 1])
        third = congruence(upper_green, window[:, 2])
        total_real = first[0] + second[0] + third[0]
        total_imag = first[1] + second[1] + third[1]
        green_function = to_bfloat(jnp.stack([total_real, total_imag], axis=2))
        complex_values = lax.complex(green_function[:, :, 0], green_function[:, :, 1])
        spectra = jnp.fft.fft(complex_values, n=PADDED, axis=1)
        correlation = jnp.fft.ifft(spectra[0] * jnp.conj(spectra[1]), axis=0)
        lag_index = jnp.arange(ENERGIES)
        lesser = correlation[:ENERGIES] * factor
        greater = jnp.conj(correlation[(PADDED - lag_index) % PADDED]) * factor
        polar = to_bfloat(jnp.stack([jnp.stack([jnp.real(lesser), jnp.imag(lesser)], axis=1), jnp.stack([jnp.real(greater), jnp.imag(greater)], axis=1)], axis=0))
        coulomb_block = lax.dynamic_index_in_dim(coulomb, block_id, 0, keepdims=False).astype(jnp.float32)
        left_product = to_bfloat(jnp.einsum('pq,fetqr->fetpr', coulomb_block, polar))
        return jnp.einsum('fetpr,sr->fetps', left_product, coulomb_block).astype(jnp.bfloat16)

    stacked = lax.map(one_block, jnp.arange(NBLOCKS, dtype=jnp.int32))
    return jnp.moveaxis(stacked, 0, 1)
```

```python
import math

import jax
import jax.numpy as jnp
from jax import lax
from jax.sharding import PartitionSpec as P


def padded_2(shard, sides, width):
    for axis, dim in sides:
        peers, length = (lax.axis_size(axis), shard.shape[dim])
        up = [(i, (i + 1) % peers) for i in range(peers - 1)]
        down = [(j, i) for i, j in up]
        last = lax.slice_in_dim(shard, length - width, length, axis=dim)
        initial = lax.slice_in_dim(shard, 0, width, axis=dim)
        before = lax.ppermute(last, axis, up)
        after = lax.ppermute(initial, axis, down)
        shard = jnp.concatenate([before, shard, after], axis=dim)
    return shard


def in_blocks(shard, dim, peers):
    before, after = (shard.shape[:dim], shard.shape[dim + 1 :])
    return jnp.moveaxis(shard.reshape(*before, peers, -1, *after), dim, 0)


def edges_of(length, count):
    unit = 8 if length >= 8 * count else 1
    return [length // unit * k // count * unit for k in range(1, count)]


def joined_along(tiles, dim):
    tiles = jnp.moveaxis(tiles, 0, dim)
    shape = tiles.shape
    return tiles.reshape(*shape[:dim], shape[dim] * shape[dim + 1], *shape[dim + 2 :])


def cut_exchange(shard, axis, pieces, split_dim, concat_dim):
    tiles = in_blocks(shard, split_dim, lax.axis_size(axis))
    split_at = max(range(1, max(2, tiles.ndim - 1)), key=lambda d: tiles.shape[d])
    gathered = []
    for slab in jnp.split(tiles, edges_of(tiles.shape[split_at], pieces), axis=split_at):
        if slab.size:
            gathered.append(lax.all_to_all(slab, axis, split_axis=0, concat_axis=0, tiled=True))
    return joined_along(jnp.concatenate(gathered, axis=split_at), concat_dim)


def congruence(green, sigma):
    green_real = green[:, :, 0]
    green_imag = green[:, :, 1]
    sigma_real = sigma[:, :, :, 0]
    sigma_imag = sigma[:, :, :, 1]
    green_wide = jnp.concatenate([green_real, green_imag], axis=-1)
    sigma_tall = jnp.concatenate(
        [
            jnp.concatenate([sigma_real, sigma_imag], axis=-1),
            jnp.concatenate([-sigma_imag, sigma_real], axis=-1),
        ],
        axis=-2,
    )
    mixed = jnp.einsum(
        "nepq,fneqr->fnepr", green_wide, sigma_tall, preferred_element_type=jnp.float32
    ).astype(jnp.bfloat16)
    adjoint_tall = jnp.concatenate(
        [green_wide, jnp.concatenate([-green_imag, green_real], axis=-1)], axis=-2
    )
    return jnp.einsum("fnepr,nesr->fneps", mixed, adjoint_tall, preferred_element_type=jnp.float32)


def split_table(table):
    high_part = table.astype(jnp.bfloat16)
    low_part = (table - high_part.astype(jnp.float32)).astype(jnp.bfloat16)
    return (high_part, low_part)


def spectrum(values, table_high, table_low, padded_len):

    def apply_table(part):
        return jnp.dot(table_high, part, preferred_element_type=jnp.float32) + jnp.dot(
            table_low, part, preferred_element_type=jnp.float32
        )

    real_terms = apply_table(values[:, 0])
    imag_terms = apply_table(values[:, 1])
    out_real = real_terms[:padded_len] + imag_terms[padded_len:]
    out_imag = imag_terms[:padded_len] - real_terms[padded_len:]
    return (out_real, out_imag)


def body(green_lower, green_diag, green_upper, self_energy, coulomb):
    block_count = green_diag.shape[0]
    energy_local = green_diag.shape[1]
    block_order = green_diag.shape[-1]
    energies = energy_local * lax.axis_size("energy")
    padded_len = 2 * energies
    padded = padded_2(self_energy, (("space", 1),), 1)
    lower_term = congruence(green_lower, padded[:, :block_count])
    diag_term = congruence(green_diag, padded[:, 1 : block_count + 1])
    upper_term = congruence(green_upper, padded[:, 2:])
    total = lower_term + diag_term + upper_term
    total = total.reshape(2, block_count, energy_local, block_order, 2, block_order)
    green_function = (
        jnp.transpose(total, (0, 2, 4, 1, 3, 5))
        .astype(jnp.bfloat16)
        .reshape(2, energy_local, 2, -1)
    )
    frequency = lax.iota(jnp.int32, padded_len)
    energy_index = lax.iota(jnp.int32, energies)
    step_angle = 2.0 * math.pi / padded_len
    forward_angle = (frequency[:, None] * energy_index[None, :] % padded_len).astype(
        jnp.float32
    ) * step_angle
    forward_table = jnp.concatenate([jnp.cos(forward_angle), jnp.sin(forward_angle)], axis=0)
    table_high, table_low = split_table(forward_table)
    entries = cut_exchange(green_function, "energy", 1, 3, 1)
    lesser_values = entries[0]
    greater_values = entries[1]
    lesser_real, lesser_imag = spectrum(lesser_values, table_high, table_low, padded_len)
    greater_real, greater_imag = spectrum(greater_values, table_high, table_low, padded_len)
    product_real = lesser_real * greater_real + lesser_imag * greater_imag
    product_imag = lesser_imag * greater_real - lesser_real * greater_imag
    row_index = jnp.concatenate([energy_index, (padded_len - energy_index) % padded_len])
    back_angle = (row_index[:, None] * frequency[None, :] % padded_len).astype(
        jnp.float32
    ) * step_angle
    back_cos = jnp.cos(back_angle)
    back_sin = jnp.sin(back_angle)
    back_table = jnp.concatenate(
        [
            jnp.concatenate([back_cos, -back_sin], axis=1),
            jnp.concatenate([back_sin, back_cos], axis=1),
        ],
        axis=0,
    )
    stacked_product = jnp.concatenate([product_real, product_imag], axis=0)
    factor = 1.0 / (padded_len * math.sqrt(energies))
    combined = (
        jnp.dot(
            back_table,
            stacked_product,
            precision=lax.Precision.HIGH,
            preferred_element_type=jnp.float32,
        )
        * factor
    )
    corr_real = combined[:padded_len]
    corr_imag = combined[padded_len:]
    lesser_lags = jnp.stack([corr_real[:energies], corr_imag[:energies]], axis=1)
    greater_lags = jnp.stack([corr_real[energies:], -corr_imag[energies:]], axis=1)
    polar = jnp.stack([lesser_lags, greater_lags], axis=0).astype(jnp.bfloat16)
    returned = lax.all_to_all(polar, "energy", split_axis=1, concat_axis=3, tiled=True)
    returned = returned.reshape(2, energy_local, 2, block_count, block_order, block_order)
    left_product = jnp.einsum(
        "npq,fetnqr->fetnpr", coulomb, returned, preferred_element_type=jnp.float32
    ).astype(jnp.bfloat16)
    screened = jnp.einsum(
        "fetnpr,nsr->fnetps", left_product, coulomb, preferred_element_type=jnp.float32
    )
    return screened.astype(jnp.bfloat16)


def solution(mesh):
    in_specs = (
        P("space", "energy", None, None, None),
        P("space", "energy", None, None, None),
        P("space", "energy", None, None, None),
        P(None, "space", "energy", None, None, None),
        P("space", None, None),
    )
    out_specs = P(None, "space", "energy", None, None, None)
    return jax.shard_map(body, mesh=mesh, in_specs=in_specs, out_specs=out_specs, check_vma=False)
```

```python
import math

import jax
import jax.numpy as jnp
from jax import lax
from jax.sharding import PartitionSpec as P


def padded_2(shard, sides, width):
    for axis, dim in sides:
        peers, length = (lax.axis_size(axis), shard.shape[dim])
        up = [(i, (i + 1) % peers) for i in range(peers - 1)]
        down = [(j, i) for i, j in up]
        last = lax.slice_in_dim(shard, length - width, length, axis=dim)
        initial = lax.slice_in_dim(shard, 0, width, axis=dim)
        before = lax.ppermute(last, axis, up)
        after = lax.ppermute(initial, axis, down)
        shard = jnp.concatenate([before, shard, after], axis=dim)
    return shard


def in_blocks(shard, dim, peers):
    before, after = (shard.shape[:dim], shard.shape[dim + 1 :])
    return jnp.moveaxis(shard.reshape(*before, peers, -1, *after), dim, 0)


def edges_of(length, count):
    unit = 8 if length >= 8 * count else 1
    return [length // unit * k // count * unit for k in range(1, count)]


def joined_along(tiles, dim):
    tiles = jnp.moveaxis(tiles, 0, dim)
    shape = tiles.shape
    return tiles.reshape(*shape[:dim], shape[dim] * shape[dim + 1], *shape[dim + 2 :])


def cut_exchange(shard, axis, pieces, split_dim, concat_dim):
    tiles = in_blocks(shard, split_dim, lax.axis_size(axis))
    split_at = max(range(1, max(2, tiles.ndim - 1)), key=lambda d: tiles.shape[d])
    gathered = []
    for slab in jnp.split(tiles, edges_of(tiles.shape[split_at], pieces), axis=split_at):
        if slab.size:
            gathered.append(lax.all_to_all(slab, axis, split_axis=0, concat_axis=0, tiled=True))
    return joined_along(jnp.concatenate(gathered, axis=split_at), concat_dim)


def congruence(green, sigma):
    green_real = green[:, :, 0]
    green_imag = green[:, :, 1]
    sigma_real = sigma[:, :, :, 0]
    sigma_imag = sigma[:, :, :, 1]
    green_wide = jnp.concatenate([green_real, green_imag], axis=-1)
    sigma_tall = jnp.concatenate(
        [
            jnp.concatenate([sigma_real, sigma_imag], axis=-1),
            jnp.concatenate([-sigma_imag, sigma_real], axis=-1),
        ],
        axis=-2,
    )
    mixed = jnp.einsum(
        "nepq,fneqr->fnepr", green_wide, sigma_tall, preferred_element_type=jnp.float32
    ).astype(jnp.bfloat16)
    adjoint_tall = jnp.concatenate(
        [green_wide, jnp.concatenate([-green_imag, green_real], axis=-1)], axis=-2
    )
    return jnp.einsum("fnepr,nesr->fneps", mixed, adjoint_tall, preferred_element_type=jnp.float32)


def split_table(table):
    high_part = table.astype(jnp.bfloat16)
    low_part = (table - high_part.astype(jnp.float32)).astype(jnp.bfloat16)
    return (high_part, low_part)


def spectrum(values, table_high, table_low, padded_len):

    def apply_table(part):
        return jnp.dot(table_high, part, preferred_element_type=jnp.float32) + jnp.dot(
            table_low, part, preferred_element_type=jnp.float32
        )

    real_terms = apply_table(values[:, 0])
    imag_terms = apply_table(values[:, 1])
    out_real = real_terms[:padded_len] + imag_terms[padded_len:]
    out_imag = imag_terms[:padded_len] - real_terms[padded_len:]
    return (out_real, out_imag)


def body(green_lower, green_diag, green_upper, self_energy, coulomb):
    block_count = green_diag.shape[0]
    energy_local = green_diag.shape[1]
    block_order = green_diag.shape[-1]
    energies = energy_local * lax.axis_size("energy")
    padded_len = 2 * energies
    peers = lax.axis_size("space")
    on_chip = [(i, i ^ 1) for i in range(peers - peers % 2)]
    across = [(i, i + 1) for i in range(1, peers - 1, 2)]
    across = across + [(j, i) for i, j in across]
    partner = lax.ppermute(self_energy, "space", on_chip)
    neighbour = lax.ppermute(self_energy, "space", across)
    even = lax.axis_index("space") % 2 == 0
    green_on = jnp.where(even, green_upper, green_lower)
    green_across = jnp.where(even, green_lower, green_upper)
    diag_term = congruence(green_diag, self_energy)
    on_term = congruence(green_on, partner)
    across_term = congruence(green_across, neighbour)
    total = diag_term + on_term + across_term
    total = total.reshape(2, block_count, energy_local, block_order, 2, block_order)
    green_function = (
        jnp.transpose(total, (0, 2, 4, 1, 3, 5))
        .astype(jnp.bfloat16)
        .reshape(2, energy_local, 2, -1)
    )
    frequency = lax.iota(jnp.int32, padded_len)
    energy_index = lax.iota(jnp.int32, energies)
    step_angle = 2.0 * math.pi / padded_len
    forward_angle = (frequency[:, None] * energy_index[None, :] % padded_len).astype(
        jnp.float32
    ) * step_angle
    forward_table = jnp.concatenate([jnp.cos(forward_angle), jnp.sin(forward_angle)], axis=0)
    table_high, table_low = split_table(forward_table)
    entries = cut_exchange(green_function, "energy", 1, 3, 1)
    lesser_values = entries[0]
    greater_values = entries[1]
    lesser_real, lesser_imag = spectrum(lesser_values, table_high, table_low, padded_len)
    greater_real, greater_imag = spectrum(greater_values, table_high, table_low, padded_len)
    product_real = lesser_real * greater_real + lesser_imag * greater_imag
    product_imag = lesser_imag * greater_real - lesser_real * greater_imag
    row_index = jnp.concatenate([energy_index, (padded_len - energy_index) % padded_len])
    back_angle = (row_index[:, None] * frequency[None, :] % padded_len).astype(
        jnp.float32
    ) * step_angle
    back_cos = jnp.cos(back_angle)
    back_sin = jnp.sin(back_angle)
    back_table = jnp.concatenate(
        [
            jnp.concatenate([back_cos, -back_sin], axis=1),
            jnp.concatenate([back_sin, back_cos], axis=1),
        ],
        axis=0,
    )
    stacked_product = jnp.concatenate([product_real, product_imag], axis=0)
    factor = 1.0 / (padded_len * math.sqrt(energies))
    combined = (
        jnp.dot(
            back_table,
            stacked_product,
            precision=lax.Precision.HIGH,
            preferred_element_type=jnp.float32,
        )
        * factor
    )
    corr_real = combined[:padded_len]
    corr_imag = combined[padded_len:]
    lesser_lags = jnp.stack([corr_real[:energies], corr_imag[:energies]], axis=1)
    greater_lags = jnp.stack([corr_real[energies:], -corr_imag[energies:]], axis=1)
    polar = jnp.stack([lesser_lags, greater_lags], axis=0).astype(jnp.bfloat16)
    returned = lax.all_to_all(polar, "energy", split_axis=1, concat_axis=3, tiled=True)
    returned = returned.reshape(2, energy_local, 2, block_count, block_order, block_order)
    left_product = jnp.einsum(
        "npq,fetnqr->fetnpr", coulomb, returned, preferred_element_type=jnp.float32
    ).astype(jnp.bfloat16)
    screened = jnp.einsum(
        "fetnpr,nsr->fnetps", left_product, coulomb, preferred_element_type=jnp.float32
    )
    return screened.astype(jnp.bfloat16)


def solution(mesh):
    in_specs = (
        P("space", "energy", None, None, None),
        P("space", "energy", None, None, None),
        P("space", "energy", None, None, None),
        P(None, "space", "energy", None, None, None),
        P("space", None, None),
    )
    out_specs = P(None, "space", "energy", None, None, None)
    return jax.shard_map(body, mesh=mesh, in_specs=in_specs, out_specs=out_specs, check_vma=False)
```

```python
import math

import jax
import jax.numpy as jnp
from jax import lax
from jax.sharding import PartitionSpec as P


def padded_2(shard, sides, width):
    for axis, dim in sides:
        peers, length = (lax.axis_size(axis), shard.shape[dim])
        up = [(i, (i + 1) % peers) for i in range(peers - 1)]
        down = [(j, i) for i, j in up]
        last = lax.slice_in_dim(shard, length - width, length, axis=dim)
        initial = lax.slice_in_dim(shard, 0, width, axis=dim)
        before = lax.ppermute(last, axis, up)
        after = lax.ppermute(initial, axis, down)
        shard = jnp.concatenate([before, shard, after], axis=dim)
    return shard


def in_blocks(shard, dim, peers):
    before, after = (shard.shape[:dim], shard.shape[dim + 1 :])
    return jnp.moveaxis(shard.reshape(*before, peers, -1, *after), dim, 0)


def edges_of(length, count):
    unit = 8 if length >= 8 * count else 1
    return [length // unit * k // count * unit for k in range(1, count)]


def joined_along(tiles, dim):
    tiles = jnp.moveaxis(tiles, 0, dim)
    shape = tiles.shape
    return tiles.reshape(*shape[:dim], shape[dim] * shape[dim + 1], *shape[dim + 2 :])


def cut_exchange(shard, axis, pieces, split_dim, concat_dim):
    tiles = in_blocks(shard, split_dim, lax.axis_size(axis))
    split_at = max(range(1, max(2, tiles.ndim - 1)), key=lambda d: tiles.shape[d])
    gathered = []
    for slab in jnp.split(tiles, edges_of(tiles.shape[split_at], pieces), axis=split_at):
        if slab.size:
            gathered.append(lax.all_to_all(slab, axis, split_axis=0, concat_axis=0, tiled=True))
    return joined_along(jnp.concatenate(gathered, axis=split_at), concat_dim)


def congruence(green, sigma):
    green_real = green[:, :, 0]
    green_imag = green[:, :, 1]
    sigma_real = sigma[:, :, :, 0]
    sigma_imag = sigma[:, :, :, 1]
    green_wide = jnp.concatenate([green_real, green_imag], axis=-1)
    sigma_tall = jnp.concatenate(
        [
            jnp.concatenate([sigma_real, sigma_imag], axis=-1),
            jnp.concatenate([-sigma_imag, sigma_real], axis=-1),
        ],
        axis=-2,
    )
    mixed = jnp.einsum(
        "nepq,fneqr->fnepr", green_wide, sigma_tall, preferred_element_type=jnp.float32
    ).astype(jnp.bfloat16)
    adjoint_tall = jnp.concatenate(
        [green_wide, jnp.concatenate([-green_imag, green_real], axis=-1)], axis=-2
    )
    return jnp.einsum("fnepr,nesr->fneps", mixed, adjoint_tall, preferred_element_type=jnp.float32)


def split_table(table):
    high_part = table.astype(jnp.bfloat16)
    low_part = (table - high_part.astype(jnp.float32)).astype(jnp.bfloat16)
    return (high_part, low_part)


def spectrum(values, table_high, table_low, padded_len):

    def apply_table(part):
        return jnp.dot(table_high, part, preferred_element_type=jnp.float32) + jnp.dot(
            table_low, part, preferred_element_type=jnp.float32
        )

    real_terms = apply_table(values[:, 0])
    imag_terms = apply_table(values[:, 1])
    out_real = real_terms[:padded_len] + imag_terms[padded_len:]
    out_imag = imag_terms[:padded_len] - real_terms[padded_len:]
    return (out_real, out_imag)


def body(green_lower, green_diag, green_upper, self_energy, coulomb):
    block_count = green_diag.shape[0]
    energy_local = green_diag.shape[1]
    block_order = green_diag.shape[-1]
    energies = energy_local * lax.axis_size("energy")
    padded_len = 2 * energies
    peers = lax.axis_size("space")
    on_chip = [(i, i ^ 1) for i in range(peers - peers % 2)]
    across = [(i, i + 1) for i in range(1, peers - 1, 2)]
    across = across + [(j, i) for i, j in across]
    partner = lax.ppermute(self_energy, "space", on_chip)
    neighbour = lax.ppermute(self_energy, "space", across)
    even = lax.axis_index("space") % 2 == 0
    green_on = jnp.where(even, green_upper, green_lower)
    green_across = jnp.where(even, green_lower, green_upper)
    diag_term = congruence(green_diag, self_energy)
    on_term = congruence(green_on, partner)
    across_term = congruence(green_across, neighbour)
    total = diag_term + on_term + across_term
    total = total.reshape(2, block_count, energy_local, block_order, 2, block_order)
    green_function = (
        jnp.transpose(total, (0, 2, 4, 1, 3, 5))
        .astype(jnp.bfloat16)
        .reshape(2, energy_local, 2, -1)
    )
    frequency = lax.iota(jnp.int32, padded_len)
    energy_index = lax.iota(jnp.int32, energies)
    step_angle = 2.0 * math.pi / padded_len
    forward_angle = (frequency[:, None] * energy_index[None, :] % padded_len).astype(
        jnp.float32
    ) * step_angle
    forward_table = jnp.concatenate([jnp.cos(forward_angle), jnp.sin(forward_angle)], axis=0)
    entries = cut_exchange(green_function, "energy", 1, 3, 1)
    spectra = jnp.einsum(
        "qe,fern->qfrn",
        forward_table.astype(jnp.bfloat16),
        entries,
        preferred_element_type=jnp.float32,
    )
    cos_part = spectra[:padded_len]
    sin_part = spectra[padded_len:]
    spec_real = cos_part[:, :, 0] + sin_part[:, :, 1]
    spec_imag = cos_part[:, :, 1] - sin_part[:, :, 0]
    product_real = spec_real[:, 0] * spec_real[:, 1] + spec_imag[:, 0] * spec_imag[:, 1]
    product_imag = spec_imag[:, 0] * spec_real[:, 1] - spec_real[:, 0] * spec_imag[:, 1]
    stacked_product = jnp.concatenate([product_real, product_imag], axis=0)
    mirrored = (padded_len - energy_index) % padded_len

    def back_rows(lags):
        angle = (lags[:, None] * frequency[None, :] % padded_len).astype(jnp.float32) * step_angle
        cos_rows, sin_rows = jnp.cos(angle), jnp.sin(angle)
        real_rows = jnp.concatenate([cos_rows, -sin_rows], axis=1)
        imag_rows = jnp.concatenate([sin_rows, cos_rows], axis=1)
        return real_rows, imag_rows

    lesser_real, lesser_imag = back_rows(energy_index)
    greater_real, greater_imag = back_rows(mirrored)
    back_table = jnp.stack([lesser_real, lesser_imag, greater_real, -greater_imag], axis=1)
    back_table = back_table.reshape(4 * energies, 2 * padded_len)
    factor = 1.0 / (padded_len * math.sqrt(energies))
    combined = jnp.dot(
        back_table.astype(jnp.bfloat16),
        stacked_product.astype(jnp.bfloat16),
        preferred_element_type=jnp.float32,
    )
    polar = (combined * factor).reshape(energies, 2, 2, -1)
    polar = jnp.transpose(polar, (1, 0, 2, 3)).astype(jnp.bfloat16)
    returned = lax.all_to_all(polar, "energy", split_axis=1, concat_axis=3, tiled=True)
    returned = returned.reshape(2, energy_local, 2, block_count, block_order, block_order)
    left_product = jnp.einsum(
        "npq,fetnqr->fetnpr", coulomb, returned, preferred_element_type=jnp.float32
    ).astype(jnp.bfloat16)
    screened = jnp.einsum(
        "fetnpr,nsr->fnetps", left_product, coulomb, preferred_element_type=jnp.float32
    )
    return screened.astype(jnp.bfloat16)


def solution(mesh):
    in_specs = (
        P("space", "energy", None, None, None),
        P("space", "energy", None, None, None),
        P("space", "energy", None, None, None),
        P(None, "space", "energy", None, None, None),
        P("space", None, None),
    )
    out_specs = P(None, "space", "energy", None, None, None)
    return jax.shard_map(body, mesh=mesh, in_specs=in_specs, out_specs=out_specs, check_vma=False)
```

```python
import math

import jax
import jax.numpy as jnp
from jax import lax
from jax.sharding import PartitionSpec as P


def padded_2(shard, sides, width):
    for axis, dim in sides:
        peers, length = (lax.axis_size(axis), shard.shape[dim])
        up = [(i, (i + 1) % peers) for i in range(peers - 1)]
        down = [(j, i) for i, j in up]
        last = lax.slice_in_dim(shard, length - width, length, axis=dim)
        initial = lax.slice_in_dim(shard, 0, width, axis=dim)
        before = lax.ppermute(last, axis, up)
        after = lax.ppermute(initial, axis, down)
        shard = jnp.concatenate([before, shard, after], axis=dim)
    return shard


def in_blocks(shard, dim, peers):
    before, after = (shard.shape[:dim], shard.shape[dim + 1 :])
    return jnp.moveaxis(shard.reshape(*before, peers, -1, *after), dim, 0)


def edges_of(length, count):
    unit = 8 if length >= 8 * count else 1
    return [length // unit * k // count * unit for k in range(1, count)]


def joined_along(tiles, dim):
    tiles = jnp.moveaxis(tiles, 0, dim)
    shape = tiles.shape
    return tiles.reshape(*shape[:dim], shape[dim] * shape[dim + 1], *shape[dim + 2 :])


def cut_exchange(shard, axis, pieces, split_dim, concat_dim):
    tiles = in_blocks(shard, split_dim, lax.axis_size(axis))
    split_at = max(range(1, max(2, tiles.ndim - 1)), key=lambda d: tiles.shape[d])
    gathered = []
    for slab in jnp.split(tiles, edges_of(tiles.shape[split_at], pieces), axis=split_at):
        if slab.size:
            gathered.append(lax.all_to_all(slab, axis, split_axis=0, concat_axis=0, tiled=True))
    return joined_along(jnp.concatenate(gathered, axis=split_at), concat_dim)


def congruence(green, sigma):
    green_real = green[:, :, 0]
    green_imag = green[:, :, 1]
    sigma_real = sigma[:, :, :, 0]
    sigma_imag = sigma[:, :, :, 1]
    green_wide = jnp.concatenate([green_real, green_imag], axis=-1)
    sigma_tall = jnp.concatenate(
        [
            jnp.concatenate([sigma_real, sigma_imag], axis=-1),
            jnp.concatenate([-sigma_imag, sigma_real], axis=-1),
        ],
        axis=-2,
    )
    mixed = jnp.einsum(
        "nepq,fneqr->fnepr", green_wide, sigma_tall, preferred_element_type=jnp.float32
    ).astype(jnp.bfloat16)
    adjoint_tall = jnp.concatenate(
        [green_wide, jnp.concatenate([-green_imag, green_real], axis=-1)], axis=-2
    )
    return jnp.einsum("fnepr,nesr->fneps", mixed, adjoint_tall, preferred_element_type=jnp.float32)


def split_table(table):
    high_part = table.astype(jnp.bfloat16)
    low_part = (table - high_part.astype(jnp.float32)).astype(jnp.bfloat16)
    return (high_part, low_part)


def spectrum(values, table_high, table_low, padded_len):

    def apply_table(part):
        return jnp.dot(table_high, part, preferred_element_type=jnp.float32) + jnp.dot(
            table_low, part, preferred_element_type=jnp.float32
        )

    real_terms = apply_table(values[:, 0])
    imag_terms = apply_table(values[:, 1])
    out_real = real_terms[:padded_len] + imag_terms[padded_len:]
    out_imag = imag_terms[:padded_len] - real_terms[padded_len:]
    return (out_real, out_imag)


def body(green_lower, green_diag, green_upper, self_energy, coulomb):
    block_count = green_diag.shape[0]
    energy_local = green_diag.shape[1]
    block_order = green_diag.shape[-1]
    energies = energy_local * lax.axis_size("energy")
    padded_len = 2 * energies
    peers = lax.axis_size("space")
    on_chip = [(i, i ^ 1) for i in range(peers - peers % 2)]
    across = [(i, i + 1) for i in range(1, peers - 1, 2)]
    across = across + [(j, i) for i, j in across]
    partner = lax.ppermute(self_energy, "space", on_chip)
    neighbour = lax.ppermute(self_energy, "space", across)
    even = lax.axis_index("space") % 2 == 0
    green_on = jnp.where(even, green_upper, green_lower)
    green_across = jnp.where(even, green_lower, green_upper)
    diag_term = congruence(green_diag, self_energy)
    on_term = congruence(green_on, partner)
    across_term = congruence(green_across, neighbour)
    total = diag_term + on_term + across_term
    groups = lax.axis_size("energy")
    total = total.reshape(2, block_count, energy_local, groups, block_order // groups, 2, block_order)
    outgoing = jnp.transpose(total, (3, 0, 2, 5, 1, 4, 6)).astype(jnp.bfloat16)
    outgoing = outgoing.reshape(groups, 2, energy_local, 2, -1)
    frequency = lax.iota(jnp.int32, padded_len)
    energy_index = lax.iota(jnp.int32, energies)
    step_angle = 2.0 * math.pi / padded_len
    forward_angle = (frequency[:, None] * energy_index[None, :] % padded_len).astype(
        jnp.float32
    ) * step_angle
    forward_table = jnp.concatenate([jnp.cos(forward_angle), jnp.sin(forward_angle)], axis=0)
    entries = lax.all_to_all(outgoing, "energy", 0, 0, tiled=True)
    spectra = jnp.einsum(
        "qxe,xfern->qfrn",
        forward_table.astype(jnp.bfloat16).reshape(2 * padded_len, groups, energy_local),
        entries,
        preferred_element_type=jnp.float32,
    )
    cos_part = spectra[:padded_len]
    sin_part = spectra[padded_len:]
    spec_real = cos_part[:, :, 0] + sin_part[:, :, 1]
    spec_imag = cos_part[:, :, 1] - sin_part[:, :, 0]
    product_real = spec_real[:, 0] * spec_real[:, 1] + spec_imag[:, 0] * spec_imag[:, 1]
    product_imag = spec_imag[:, 0] * spec_real[:, 1] - spec_real[:, 0] * spec_imag[:, 1]
    stacked_product = jnp.concatenate([product_real, product_imag], axis=0)
    mirrored = (padded_len - energy_index) % padded_len

    def back_rows(lags):
        angle = (lags[:, None] * frequency[None, :] % padded_len).astype(jnp.float32) * step_angle
        cos_rows, sin_rows = jnp.cos(angle), jnp.sin(angle)
        real_rows = jnp.concatenate([cos_rows, -sin_rows], axis=1)
        imag_rows = jnp.concatenate([sin_rows, cos_rows], axis=1)
        return real_rows, imag_rows

    lesser_real, lesser_imag = back_rows(energy_index)
    greater_real, greater_imag = back_rows(mirrored)
    back_table = jnp.stack([lesser_real, lesser_imag, greater_real, -greater_imag], axis=1)
    back_table = back_table.reshape(4 * energies, 2 * padded_len)
    factor = 1.0 / (padded_len * math.sqrt(energies))
    combined = jnp.dot(
        back_table.astype(jnp.bfloat16),
        stacked_product.astype(jnp.bfloat16),
        preferred_element_type=jnp.float32,
    )
    polar = (combined * factor).astype(jnp.bfloat16).reshape(groups, energy_local, 2, 2, -1)
    returned = lax.all_to_all(polar, "energy", 0, 0, tiled=True)
    returned = returned.reshape(groups, energy_local, 2, 2, block_count, -1, block_order)
    returned = jnp.transpose(returned, (2, 1, 3, 4, 0, 5, 6))
    returned = returned.reshape(2, energy_local, 2, block_count, block_order, block_order)
    left_product = jnp.einsum(
        "npq,fetnqr->fetnpr", coulomb, returned, preferred_element_type=jnp.float32
    ).astype(jnp.bfloat16)
    screened = jnp.einsum(
        "fetnpr,nsr->fnetps", left_product, coulomb, preferred_element_type=jnp.float32
    )
    return screened.astype(jnp.bfloat16)


def solution(mesh):
    in_specs = (
        P("space", "energy", None, None, None),
        P("space", "energy", None, None, None),
        P("space", "energy", None, None, None),
        P(None, "space", "energy", None, None, None),
        P("space", None, None),
    )
    out_specs = P(None, "space", "energy", None, None, None)
    return jax.shard_map(body, mesh=mesh, in_specs=in_specs, out_specs=out_specs, check_vma=False)
```

```python
import math

import jax
import jax.numpy as jnp
from jax import lax
from jax.sharding import PartitionSpec as P


def padded_2(shard, sides, width):
    for axis, dim in sides:
        peers, length = (lax.axis_size(axis), shard.shape[dim])
        up = [(i, (i + 1) % peers) for i in range(peers - 1)]
        down = [(j, i) for i, j in up]
        last = lax.slice_in_dim(shard, length - width, length, axis=dim)
        initial = lax.slice_in_dim(shard, 0, width, axis=dim)
        before = lax.ppermute(last, axis, up)
        after = lax.ppermute(initial, axis, down)
        shard = jnp.concatenate([before, shard, after], axis=dim)
    return shard


def in_blocks(shard, dim, peers):
    before, after = (shard.shape[:dim], shard.shape[dim + 1 :])
    return jnp.moveaxis(shard.reshape(*before, peers, -1, *after), dim, 0)


def edges_of(length, count):
    unit = 8 if length >= 8 * count else 1
    return [length // unit * k // count * unit for k in range(1, count)]


def joined_along(tiles, dim):
    tiles = jnp.moveaxis(tiles, 0, dim)
    shape = tiles.shape
    return tiles.reshape(*shape[:dim], shape[dim] * shape[dim + 1], *shape[dim + 2 :])


def cut_exchange(shard, axis, pieces, split_dim, concat_dim):
    tiles = in_blocks(shard, split_dim, lax.axis_size(axis))
    split_at = max(range(1, max(2, tiles.ndim - 1)), key=lambda d: tiles.shape[d])
    gathered = []
    for slab in jnp.split(tiles, edges_of(tiles.shape[split_at], pieces), axis=split_at):
        if slab.size:
            gathered.append(lax.all_to_all(slab, axis, split_axis=0, concat_axis=0, tiled=True))
    return joined_along(jnp.concatenate(gathered, axis=split_at), concat_dim)


def congruence(green, sigma):
    green_real = green[:, :, 0]
    green_imag = green[:, :, 1]
    sigma_real = sigma[:, :, :, 0]
    sigma_imag = sigma[:, :, :, 1]
    green_wide = jnp.concatenate([green_real, green_imag], axis=-1)
    sigma_tall = jnp.concatenate(
        [
            jnp.concatenate([sigma_real, sigma_imag], axis=-1),
            jnp.concatenate([-sigma_imag, sigma_real], axis=-1),
        ],
        axis=-2,
    )
    mixed = jnp.einsum(
        "nepq,fneqr->fnepr", green_wide, sigma_tall, preferred_element_type=jnp.float32
    ).astype(jnp.bfloat16)
    adjoint_tall = jnp.concatenate(
        [green_wide, jnp.concatenate([-green_imag, green_real], axis=-1)], axis=-2
    )
    return jnp.einsum("fnepr,nesr->fneps", mixed, adjoint_tall, preferred_element_type=jnp.float32)


def split_table(table):
    high_part = table.astype(jnp.bfloat16)
    low_part = (table - high_part.astype(jnp.float32)).astype(jnp.bfloat16)
    return (high_part, low_part)


def spectrum(values, table_high, table_low, padded_len):

    def apply_table(part):
        return jnp.dot(table_high, part, preferred_element_type=jnp.float32) + jnp.dot(
            table_low, part, preferred_element_type=jnp.float32
        )

    real_terms = apply_table(values[:, 0])
    imag_terms = apply_table(values[:, 1])
    out_real = real_terms[:padded_len] + imag_terms[padded_len:]
    out_imag = imag_terms[:padded_len] - real_terms[padded_len:]
    return (out_real, out_imag)


def body(green_lower, green_diag, green_upper, self_energy, coulomb):
    block_count = green_diag.shape[0]
    energy_local = green_diag.shape[1]
    block_order = green_diag.shape[-1]
    energies = energy_local * lax.axis_size("energy")
    padded_len = 2 * energies
    peers = lax.axis_size("space")
    on_chip = [(i, i ^ 1) for i in range(peers - peers % 2)]
    across = [(i, i + 1) for i in range(1, peers - 1, 2)]
    across = across + [(j, i) for i, j in across]
    neighbour = lax.ppermute(self_energy, "space", across)
    diag_term = congruence(green_diag, self_energy)
    own_energy, diag_term = lax.optimization_barrier((self_energy, diag_term))
    partner = lax.ppermute(own_energy, "space", on_chip)
    even = lax.axis_index("space") % 2 == 0
    green_on = jnp.where(even, green_upper, green_lower)
    green_across = jnp.where(even, green_lower, green_upper)
    near_sum = diag_term + congruence(green_on, partner)
    near_sum, neighbour = lax.optimization_barrier((near_sum, neighbour))
    across_term = congruence(green_across, neighbour)
    total = near_sum + across_term
    groups = lax.axis_size("energy")
    total = total.reshape(2, block_count, energy_local, groups, block_order // groups, 2, block_order)
    outgoing = jnp.transpose(total, (3, 0, 2, 5, 1, 4, 6)).astype(jnp.bfloat16)
    outgoing = outgoing.reshape(groups, 2, energy_local, 2, -1)
    frequency = lax.iota(jnp.int32, padded_len)
    energy_index = lax.iota(jnp.int32, energies)
    step_angle = 2.0 * math.pi / padded_len
    forward_angle = (frequency[:, None] * energy_index[None, :] % padded_len).astype(
        jnp.float32
    ) * step_angle
    forward_table = jnp.concatenate([jnp.cos(forward_angle), jnp.sin(forward_angle)], axis=0)
    entries = lax.all_to_all(outgoing, "energy", 0, 0, tiled=True)
    spectra = jnp.einsum(
        "qxe,xfern->qfrn",
        forward_table.astype(jnp.bfloat16).reshape(2 * padded_len, groups, energy_local),
        entries,
        preferred_element_type=jnp.float32,
    )
    cos_part = spectra[:padded_len]
    sin_part = spectra[padded_len:]
    spec_real = cos_part[:, :, 0] + sin_part[:, :, 1]
    spec_imag = cos_part[:, :, 1] - sin_part[:, :, 0]
    product_real = spec_real[:, 0] * spec_real[:, 1] + spec_imag[:, 0] * spec_imag[:, 1]
    product_imag = spec_imag[:, 0] * spec_real[:, 1] - spec_real[:, 0] * spec_imag[:, 1]
    stacked_product = jnp.concatenate([product_real, product_imag], axis=0)
    mirrored = (padded_len - energy_index) % padded_len

    def back_rows(lags):
        angle = (lags[:, None] * frequency[None, :] % padded_len).astype(jnp.float32) * step_angle
        cos_rows, sin_rows = jnp.cos(angle), jnp.sin(angle)
        real_rows = jnp.concatenate([cos_rows, -sin_rows], axis=1)
        imag_rows = jnp.concatenate([sin_rows, cos_rows], axis=1)
        return real_rows, imag_rows

    lesser_real, lesser_imag = back_rows(energy_index)
    greater_real, greater_imag = back_rows(mirrored)
    back_table = jnp.stack([lesser_real, lesser_imag, greater_real, -greater_imag], axis=1)
    back_table = back_table.reshape(4 * energies, 2 * padded_len)
    factor = 1.0 / (padded_len * math.sqrt(energies))
    combined = jnp.dot(
        back_table.astype(jnp.bfloat16),
        stacked_product.astype(jnp.bfloat16),
        preferred_element_type=jnp.float32,
    )
    polar = (combined * factor).astype(jnp.bfloat16).reshape(groups, energy_local, 2, 2, -1)
    returned = lax.all_to_all(polar, "energy", 0, 0, tiled=True)
    returned = returned.reshape(groups, energy_local, 2, 2, block_count, -1, block_order)
    returned = jnp.transpose(returned, (2, 1, 3, 4, 0, 5, 6))
    returned = returned.reshape(2, energy_local, 2, block_count, block_order, block_order)
    left_product = jnp.einsum(
        "npq,fetnqr->fetnpr", coulomb, returned, preferred_element_type=jnp.float32
    ).astype(jnp.bfloat16)
    screened = jnp.einsum(
        "fetnpr,nsr->fnetps", left_product, coulomb, preferred_element_type=jnp.float32
    )
    return screened.astype(jnp.bfloat16)


def solution(mesh):
    in_specs = (
        P("space", "energy", None, None, None),
        P("space", "energy", None, None, None),
        P("space", "energy", None, None, None),
        P(None, "space", "energy", None, None, None),
        P("space", None, None),
    )
    out_specs = P(None, "space", "energy", None, None, None)
    return jax.shard_map(body, mesh=mesh, in_specs=in_specs, out_specs=out_specs, check_vma=False)
```

```python
import math

import jax
import jax.numpy as jnp
from jax import lax
from jax.sharding import PartitionSpec as P


def padded_2(shard, sides, width):
    for axis, dim in sides:
        peers, length = (lax.axis_size(axis), shard.shape[dim])
        up = [(i, (i + 1) % peers) for i in range(peers - 1)]
        down = [(j, i) for i, j in up]
        last = lax.slice_in_dim(shard, length - width, length, axis=dim)
        initial = lax.slice_in_dim(shard, 0, width, axis=dim)
        before = lax.ppermute(last, axis, up)
        after = lax.ppermute(initial, axis, down)
        shard = jnp.concatenate([before, shard, after], axis=dim)
    return shard


def in_blocks(shard, dim, peers):
    before, after = (shard.shape[:dim], shard.shape[dim + 1 :])
    return jnp.moveaxis(shard.reshape(*before, peers, -1, *after), dim, 0)


def edges_of(length, count):
    unit = 8 if length >= 8 * count else 1
    return [length // unit * k // count * unit for k in range(1, count)]


def joined_along(tiles, dim):
    tiles = jnp.moveaxis(tiles, 0, dim)
    shape = tiles.shape
    return tiles.reshape(*shape[:dim], shape[dim] * shape[dim + 1], *shape[dim + 2 :])


def cut_exchange(shard, axis, pieces, split_dim, concat_dim):
    tiles = in_blocks(shard, split_dim, lax.axis_size(axis))
    split_at = max(range(1, max(2, tiles.ndim - 1)), key=lambda d: tiles.shape[d])
    gathered = []
    for slab in jnp.split(tiles, edges_of(tiles.shape[split_at], pieces), axis=split_at):
        if slab.size:
            gathered.append(lax.all_to_all(slab, axis, split_axis=0, concat_axis=0, tiled=True))
    return joined_along(jnp.concatenate(gathered, axis=split_at), concat_dim)


def congruence(green, sigma):
    green_real = green[:, :, 0]
    green_imag = green[:, :, 1]
    sigma_real = sigma[:, :, :, 0]
    sigma_imag = sigma[:, :, :, 1]
    green_wide = jnp.concatenate([green_real, green_imag], axis=-1)
    sigma_tall = jnp.concatenate(
        [
            jnp.concatenate([sigma_real, sigma_imag], axis=-1),
            jnp.concatenate([-sigma_imag, sigma_real], axis=-1),
        ],
        axis=-2,
    )
    mixed = jnp.einsum(
        "nepq,fneqr->fnepr", green_wide, sigma_tall, preferred_element_type=jnp.float32
    ).astype(jnp.bfloat16)
    adjoint_tall = jnp.concatenate(
        [green_wide, jnp.concatenate([-green_imag, green_real], axis=-1)], axis=-2
    )
    return jnp.einsum("fnepr,nesr->fneps", mixed, adjoint_tall, preferred_element_type=jnp.float32)


def split_table(table):
    high_part = table.astype(jnp.bfloat16)
    low_part = (table - high_part.astype(jnp.float32)).astype(jnp.bfloat16)
    return (high_part, low_part)


def spectrum(values, table_high, table_low, padded_len):

    def apply_table(part):
        return jnp.dot(table_high, part, preferred_element_type=jnp.float32) + jnp.dot(
            table_low, part, preferred_element_type=jnp.float32
        )

    real_terms = apply_table(values[:, 0])
    imag_terms = apply_table(values[:, 1])
    out_real = real_terms[:padded_len] + imag_terms[padded_len:]
    out_imag = imag_terms[:padded_len] - real_terms[padded_len:]
    return (out_real, out_imag)


def body(green_lower, green_diag, green_upper, self_energy, coulomb):
    block_count = green_diag.shape[0]
    energy_local = green_diag.shape[1]
    block_order = green_diag.shape[-1]
    energies = energy_local * lax.axis_size("energy")
    padded_len = 2 * energies
    peers = lax.axis_size("space")
    on_chip = [(i, i ^ 1) for i in range(peers - peers % 2)]
    across = [(i, i + 1) for i in range(1, peers - 1, 2)]
    across = across + [(j, i) for i, j in across]
    neighbour = lax.ppermute(self_energy, "space", across)
    diag_term = congruence(green_diag, self_energy)
    own_energy, diag_term = lax.optimization_barrier((self_energy, diag_term))
    partner = lax.ppermute(own_energy, "space", on_chip)
    even = lax.axis_index("space") % 2 == 0
    green_on = jnp.where(even, green_upper, green_lower)
    green_across = jnp.where(even, green_lower, green_upper)
    near_sum = diag_term + congruence(green_on, partner)
    near_sum, neighbour = lax.optimization_barrier((near_sum, neighbour))
    across_term = congruence(green_across, neighbour)
    total = near_sum + across_term
    groups = lax.axis_size("energy")
    total = total.reshape(2, block_count, energy_local, groups, block_order // groups, 2, block_order)
    outgoing = jnp.transpose(total, (3, 0, 2, 5, 1, 4, 6)).astype(jnp.bfloat16)
    outgoing = outgoing.reshape(groups, 2, energy_local, 2, -1)
    frequency = lax.iota(jnp.int32, padded_len)
    energy_index = lax.iota(jnp.int32, energies)
    step_angle = 2.0 * math.pi / padded_len
    forward_angle = (frequency[:, None] * energy_index[None, :] % padded_len).astype(
        jnp.float32
    ) * step_angle
    cos_table, sin_table = jnp.cos(forward_angle), jnp.sin(forward_angle)
    forward_table = jnp.concatenate(
        [
            jnp.stack([cos_table, sin_table], axis=-1),
            jnp.stack([-sin_table, cos_table], axis=-1),
        ],
        axis=0,
    ).astype(jnp.bfloat16)
    entries = lax.all_to_all(outgoing, "energy", 0, 0, tiled=True)
    spectra = jnp.einsum(
        "qxer,xfern->qfn",
        forward_table.reshape(2 * padded_len, groups, energy_local, 2),
        entries,
        preferred_element_type=jnp.float32,
    )
    spec_real = spectra[:padded_len]
    spec_imag = spectra[padded_len:]
    product_real = spec_real[:, 0] * spec_real[:, 1] + spec_imag[:, 0] * spec_imag[:, 1]
    product_imag = spec_imag[:, 0] * spec_real[:, 1] - spec_real[:, 0] * spec_imag[:, 1]
    stacked_product = jnp.concatenate([product_real, product_imag], axis=0)
    mirrored = (padded_len - energy_index) % padded_len

    def back_rows(lags):
        angle = (lags[:, None] * frequency[None, :] % padded_len).astype(jnp.float32) * step_angle
        cos_rows, sin_rows = jnp.cos(angle), jnp.sin(angle)
        real_rows = jnp.concatenate([cos_rows, -sin_rows], axis=1)
        imag_rows = jnp.concatenate([sin_rows, cos_rows], axis=1)
        return real_rows, imag_rows

    lesser_real, lesser_imag = back_rows(energy_index)
    greater_real, greater_imag = back_rows(mirrored)
    back_table = jnp.stack([lesser_real, lesser_imag, greater_real, -greater_imag], axis=1)
    back_table = back_table.reshape(4 * energies, 2 * padded_len)
    factor = 1.0 / (padded_len * math.sqrt(energies))
    combined = jnp.dot(
        back_table.astype(jnp.bfloat16),
        stacked_product.astype(jnp.bfloat16),
        preferred_element_type=jnp.float32,
    )
    polar = (combined * factor).astype(jnp.bfloat16).reshape(groups, energy_local, 2, 2, -1)
    returned = lax.all_to_all(polar, "energy", 0, 0, tiled=True)
    returned = returned.reshape(groups, energy_local, 2, 2, block_count, -1, block_order)
    returned = jnp.transpose(returned, (2, 1, 3, 4, 0, 5, 6))
    returned = returned.reshape(2, energy_local, 2, block_count, block_order, block_order)
    left_product = jnp.einsum(
        "npq,fetnqr->fetnpr", coulomb, returned, preferred_element_type=jnp.float32
    ).astype(jnp.bfloat16)
    screened = jnp.einsum(
        "fetnpr,nsr->fnetps", left_product, coulomb, preferred_element_type=jnp.float32
    )
    return screened.astype(jnp.bfloat16)


def solution(mesh):
    in_specs = (
        P("space", "energy", None, None, None),
        P("space", "energy", None, None, None),
        P("space", "energy", None, None, None),
        P(None, "space", "energy", None, None, None),
        P("space", None, None),
    )
    out_specs = P(None, "space", "energy", None, None, None)
    return jax.shard_map(body, mesh=mesh, in_specs=in_specs, out_specs=out_specs, check_vma=False)
```

```python
import math

import jax
import jax.numpy as jnp
from jax import lax
from jax.sharding import PartitionSpec as P


def padded_2(shard, sides, width):
    for axis, dim in sides:
        peers, length = (lax.axis_size(axis), shard.shape[dim])
        up = [(i, (i + 1) % peers) for i in range(peers - 1)]
        down = [(j, i) for i, j in up]
        last = lax.slice_in_dim(shard, length - width, length, axis=dim)
        initial = lax.slice_in_dim(shard, 0, width, axis=dim)
        before = lax.ppermute(last, axis, up)
        after = lax.ppermute(initial, axis, down)
        shard = jnp.concatenate([before, shard, after], axis=dim)
    return shard


def in_blocks(shard, dim, peers):
    before, after = (shard.shape[:dim], shard.shape[dim + 1 :])
    return jnp.moveaxis(shard.reshape(*before, peers, -1, *after), dim, 0)


def edges_of(length, count):
    unit = 8 if length >= 8 * count else 1
    return [length // unit * k // count * unit for k in range(1, count)]


def joined_along(tiles, dim):
    tiles = jnp.moveaxis(tiles, 0, dim)
    shape = tiles.shape
    return tiles.reshape(*shape[:dim], shape[dim] * shape[dim + 1], *shape[dim + 2 :])


def cut_exchange(shard, axis, pieces, split_dim, concat_dim):
    tiles = in_blocks(shard, split_dim, lax.axis_size(axis))
    split_at = max(range(1, max(2, tiles.ndim - 1)), key=lambda d: tiles.shape[d])
    gathered = []
    for slab in jnp.split(tiles, edges_of(tiles.shape[split_at], pieces), axis=split_at):
        if slab.size:
            gathered.append(lax.all_to_all(slab, axis, split_axis=0, concat_axis=0, tiled=True))
    return joined_along(jnp.concatenate(gathered, axis=split_at), concat_dim)


def congruence(green, sigma):
    green = jnp.broadcast_to(green[None], (sigma.shape[0],) + green.shape)
    product = jnp.einsum(
        "fneiqr,fnegsr->fneiqgs", sigma, green, preferred_element_type=jnp.float32
    )
    right_real = product[:, :, :, 0, :, 0] + product[:, :, :, 1, :, 1]
    right_imag = product[:, :, :, 1, :, 0] - product[:, :, :, 0, :, 1]
    right = jnp.stack([right_real, right_imag], axis=3).astype(jnp.bfloat16)
    total = jnp.einsum("fnegpq,fnecqs->fnegcps", green, right, preferred_element_type=jnp.float32)
    out_real = total[:, :, :, 0, 0] - total[:, :, :, 1, 1]
    out_imag = total[:, :, :, 0, 1] + total[:, :, :, 1, 0]
    return jnp.stack([out_real, out_imag], axis=3)


def split_table(table):
    high_part = table.astype(jnp.bfloat16)
    low_part = (table - high_part.astype(jnp.float32)).astype(jnp.bfloat16)
    return (high_part, low_part)


def spectrum(values, table_high, table_low, padded_len):

    def apply_table(part):
        return jnp.dot(table_high, part, preferred_element_type=jnp.float32) + jnp.dot(
            table_low, part, preferred_element_type=jnp.float32
        )

    real_terms = apply_table(values[:, 0])
    imag_terms = apply_table(values[:, 1])
    out_real = real_terms[:padded_len] + imag_terms[padded_len:]
    out_imag = imag_terms[:padded_len] - real_terms[padded_len:]
    return (out_real, out_imag)


def body(green_lower, green_diag, green_upper, self_energy, coulomb):
    block_count = green_diag.shape[0]
    energy_local = green_diag.shape[1]
    block_order = green_diag.shape[-1]
    energies = energy_local * lax.axis_size("energy")
    padded_len = 2 * energies
    peers = lax.axis_size("space")
    on_chip = [(i, i ^ 1) for i in range(peers - peers % 2)]
    across = [(i, i + 1) for i in range(1, peers - 1, 2)]
    across = across + [(j, i) for i, j in across]
    neighbour = lax.ppermute(self_energy, "space", across)
    partner = lax.ppermute(self_energy, "space", on_chip)
    diag_term = congruence(green_diag, self_energy)
    even = lax.axis_index("space") % 2 == 0
    green_on = jnp.where(even, green_upper, green_lower)
    green_across = jnp.where(even, green_lower, green_upper)
    near_sum = diag_term + congruence(green_on, partner)
    near_sum, neighbour = lax.optimization_barrier((near_sum, neighbour))
    across_term = congruence(green_across, neighbour)
    total = near_sum + across_term
    groups = lax.axis_size("energy")
    total = total.reshape(2, block_count, energy_local, 2, groups, block_order // groups, block_order)
    outgoing = jnp.transpose(total, (4, 0, 2, 3, 1, 5, 6)).astype(jnp.bfloat16)
    outgoing = outgoing.reshape(groups, 2, energy_local, 2, -1)
    frequency = lax.iota(jnp.int32, padded_len)
    energy_index = lax.iota(jnp.int32, energies)
    step_angle = 2.0 * math.pi / padded_len
    forward_angle = (frequency[:, None] * energy_index[None, :] % padded_len).astype(
        jnp.float32
    ) * step_angle
    cos_table, sin_table = jnp.cos(forward_angle), jnp.sin(forward_angle)
    forward_table = jnp.concatenate(
        [
            jnp.stack([cos_table, sin_table], axis=-1),
            jnp.stack([-sin_table, cos_table], axis=-1),
        ],
        axis=0,
    ).astype(jnp.bfloat16)
    entries = lax.all_to_all(outgoing, "energy", 0, 0, tiled=True)
    spectra = jnp.einsum(
        "qxer,xfern->qfn",
        forward_table.reshape(2 * padded_len, groups, energy_local, 2),
        entries,
        preferred_element_type=jnp.float32,
    )
    spec_real = spectra[:padded_len]
    spec_imag = spectra[padded_len:]
    product_real = spec_real[:, 0] * spec_real[:, 1] + spec_imag[:, 0] * spec_imag[:, 1]
    product_imag = spec_imag[:, 0] * spec_real[:, 1] - spec_real[:, 0] * spec_imag[:, 1]
    stacked_product = jnp.concatenate([product_real, product_imag], axis=0)
    mirrored = (padded_len - energy_index) % padded_len

    def back_rows(lags):
        angle = (lags[:, None] * frequency[None, :] % padded_len).astype(jnp.float32) * step_angle
        cos_rows, sin_rows = jnp.cos(angle), jnp.sin(angle)
        real_rows = jnp.concatenate([cos_rows, -sin_rows], axis=1)
        imag_rows = jnp.concatenate([sin_rows, cos_rows], axis=1)
        return real_rows, imag_rows

    lesser_real, lesser_imag = back_rows(energy_index)
    greater_real, greater_imag = back_rows(mirrored)
    back_table = jnp.stack([lesser_real, lesser_imag, greater_real, -greater_imag], axis=1)
    back_table = back_table.reshape(4 * energies, 2 * padded_len)
    factor = 1.0 / (padded_len * math.sqrt(energies))
    combined = jnp.dot(
        back_table.astype(jnp.bfloat16),
        stacked_product.astype(jnp.bfloat16),
        preferred_element_type=jnp.float32,
    )
    polar = (combined * factor).astype(jnp.bfloat16).reshape(groups, energy_local, 2, 2, -1)
    returned = lax.all_to_all(polar, "energy", 0, 0, tiled=True)
    returned = returned.reshape(groups, energy_local, 2, 2, block_count, -1, block_order)
    returned = jnp.transpose(returned, (2, 1, 3, 4, 0, 5, 6))
    returned = returned.reshape(2, energy_local, 2, block_count, block_order, block_order)
    left_product = jnp.einsum(
        "npq,fetnqr->fetnpr", coulomb, returned, preferred_element_type=jnp.float32
    ).astype(jnp.bfloat16)
    screened = jnp.einsum(
        "fetnpr,nsr->fnetps", left_product, coulomb, preferred_element_type=jnp.float32
    )
    return screened.astype(jnp.bfloat16)


def solution(mesh):
    in_specs = (
        P("space", "energy", None, None, None),
        P("space", "energy", None, None, None),
        P("space", "energy", None, None, None),
        P(None, "space", "energy", None, None, None),
        P("space", None, None),
    )
    out_specs = P(None, "space", "energy", None, None, None)
    return jax.shard_map(body, mesh=mesh, in_specs=in_specs, out_specs=out_specs, check_vma=False)
```

```python
import math

import jax
import jax.numpy as jnp
from jax import lax
from jax.sharding import PartitionSpec as P


def congruence(green, sigma):
    green = jnp.broadcast_to(green[None], (sigma.shape[0],) + green.shape)
    product = jnp.einsum(
        "fneiqr,fnegsr->fneiqgs", sigma, green, preferred_element_type=jnp.float32
    )
    right_real = product[:, :, :, 0, :, 0] + product[:, :, :, 1, :, 1]
    right_imag = product[:, :, :, 1, :, 0] - product[:, :, :, 0, :, 1]
    right = jnp.stack([right_real, right_imag], axis=3).astype(jnp.bfloat16)
    total = jnp.einsum("fnegpq,fnecqs->fnegcps", green, right, preferred_element_type=jnp.float32)
    out_real = total[:, :, :, 0, 0] - total[:, :, :, 1, 1]
    out_imag = total[:, :, :, 0, 1] + total[:, :, :, 1, 0]
    return jnp.stack([out_real, out_imag], axis=3)


def body(green_lower, green_diag, green_upper, self_energy, coulomb):
    block_count = green_diag.shape[0]
    energy_local = green_diag.shape[1]
    block_order = green_diag.shape[-1]
    energies = energy_local * lax.axis_size("energy")
    padded_len = 2 * energies
    peers = lax.axis_size("space")
    on_chip = [(i, i ^ 1) for i in range(peers - peers % 2)]
    across = [(i, i + 1) for i in range(1, peers - 1, 2)]
    across = across + [(j, i) for i, j in across]
    neighbour = lax.ppermute(self_energy, "space", across)
    partner = lax.ppermute(self_energy, "space", on_chip)
    diag_term = congruence(green_diag, self_energy)
    even = lax.axis_index("space") % 2 == 0
    green_on = jnp.where(even, green_upper, green_lower)
    green_across = jnp.where(even, green_lower, green_upper)
    near_sum = diag_term + congruence(green_on, partner)
    near_sum, neighbour = lax.optimization_barrier((near_sum, neighbour))
    across_term = congruence(green_across, neighbour)
    total = near_sum + across_term
    groups = lax.axis_size("energy")
    total = total.reshape(2, block_count, energy_local, 2, groups, block_order // groups, block_order)
    outgoing = jnp.transpose(total, (4, 0, 2, 3, 1, 5, 6)).astype(jnp.bfloat16)
    outgoing = outgoing.reshape(groups, 2, energy_local, 2, -1)
    frequency = lax.iota(jnp.int32, padded_len)
    energy_index = lax.iota(jnp.int32, energies)
    step_angle = 2.0 * math.pi / padded_len
    forward_angle = (frequency[:, None] * energy_index[None, :] % padded_len).astype(
        jnp.float32
    ) * step_angle
    cos_table, sin_table = jnp.cos(forward_angle), jnp.sin(forward_angle)
    forward_table = jnp.concatenate(
        [
            jnp.stack([cos_table, sin_table], axis=-1),
            jnp.stack([-sin_table, cos_table], axis=-1),
        ],
        axis=0,
    ).astype(jnp.bfloat16)
    entries = lax.all_to_all(outgoing, "energy", 0, 0, tiled=True)
    spectra = jnp.einsum(
        "qxer,xfern->qfn",
        forward_table.reshape(2 * padded_len, groups, energy_local, 2),
        entries,
        preferred_element_type=jnp.float32,
    )
    spec_real = spectra[:padded_len]
    spec_imag = spectra[padded_len:]
    product_real = spec_real[:, 0] * spec_real[:, 1] + spec_imag[:, 0] * spec_imag[:, 1]
    product_imag = spec_imag[:, 0] * spec_real[:, 1] - spec_real[:, 0] * spec_imag[:, 1]
    stacked_product = jnp.concatenate([product_real, product_imag], axis=0)
    mirrored = (padded_len - energy_index) % padded_len

    def back_rows(lags):
        angle = (lags[:, None] * frequency[None, :] % padded_len).astype(jnp.float32) * step_angle
        cos_rows, sin_rows = jnp.cos(angle), jnp.sin(angle)
        real_rows = jnp.concatenate([cos_rows, -sin_rows], axis=1)
        imag_rows = jnp.concatenate([sin_rows, cos_rows], axis=1)
        return real_rows, imag_rows

    lesser_real, lesser_imag = back_rows(energy_index)
    greater_real, greater_imag = back_rows(mirrored)
    back_table = jnp.stack([lesser_real, lesser_imag, greater_real, -greater_imag], axis=1)
    back_table = back_table.reshape(4 * energies, 2 * padded_len)
    factor = 1.0 / (padded_len * math.sqrt(energies))
    combined = jnp.dot(
        back_table.astype(jnp.bfloat16),
        stacked_product.astype(jnp.bfloat16),
        preferred_element_type=jnp.float32,
    )
    polar = (combined * factor).astype(jnp.bfloat16).reshape(groups, energy_local, 2, 2, -1)
    returned = lax.all_to_all(polar, "energy", 0, 0, tiled=True)
    returned = returned.reshape(groups, energy_local, 2, 2, block_count, -1, block_order)
    returned = jnp.transpose(returned, (2, 1, 3, 4, 0, 5, 6))
    returned = returned.reshape(2, energy_local, 2, block_count, block_order, block_order)
    left_product = jnp.einsum(
        "npq,fetnqr->fetnpr", coulomb, returned, preferred_element_type=jnp.float32
    ).astype(jnp.bfloat16)
    screened = jnp.einsum(
        "fetnpr,nsr->fnetps", left_product, coulomb, preferred_element_type=jnp.float32
    )
    return screened.astype(jnp.bfloat16)


def solution(mesh):
    in_specs = (
        P("space", "energy", None, None, None),
        P("space", "energy", None, None, None),
        P("space", "energy", None, None, None),
        P(None, "space", "energy", None, None, None),
        P("space", None, None),
    )
    out_specs = P(None, "space", "energy", None, None, None)
    return jax.shard_map(body, mesh=mesh, in_specs=in_specs, out_specs=out_specs, check_vma=False)
```

```python
import math

import jax
import jax.numpy as jnp
from jax import lax
from jax.sharding import PartitionSpec as P


def padded_2(shard, sides, width):
    for axis, dim in sides:
        peers, length = (lax.axis_size(axis), shard.shape[dim])
        up = [(i, (i + 1) % peers) for i in range(peers - 1)]
        down = [(j, i) for i, j in up]
        last = lax.slice_in_dim(shard, length - width, length, axis=dim)
        initial = lax.slice_in_dim(shard, 0, width, axis=dim)
        before = lax.ppermute(last, axis, up)
        after = lax.ppermute(initial, axis, down)
        shard = jnp.concatenate([before, shard, after], axis=dim)
    return shard


def in_blocks(shard, dim, peers):
    before, after = (shard.shape[:dim], shard.shape[dim + 1 :])
    return jnp.moveaxis(shard.reshape(*before, peers, -1, *after), dim, 0)


def edges_of(length, count):
    unit = 8 if length >= 8 * count else 1
    return [length // unit * k // count * unit for k in range(1, count)]


def joined_along(tiles, dim):
    tiles = jnp.moveaxis(tiles, 0, dim)
    shape = tiles.shape
    return tiles.reshape(*shape[:dim], shape[dim] * shape[dim + 1], *shape[dim + 2 :])


def cut_exchange(shard, axis, pieces, split_dim, concat_dim):
    tiles = in_blocks(shard, split_dim, lax.axis_size(axis))
    split_at = max(range(1, max(2, tiles.ndim - 1)), key=lambda d: tiles.shape[d])
    gathered = []
    for slab in jnp.split(tiles, edges_of(tiles.shape[split_at], pieces), axis=split_at):
        if slab.size:
            gathered.append(lax.all_to_all(slab, axis, split_axis=0, concat_axis=0, tiled=True))
    return joined_along(jnp.concatenate(gathered, axis=split_at), concat_dim)


def congruence(green, sigma):
    green = jnp.broadcast_to(green[None], (sigma.shape[0],) + green.shape)
    product = jnp.einsum(
        "fneiqr,fnegsr->fneiqgs", sigma, green, preferred_element_type=jnp.float32
    )
    right_real = product[:, :, :, 0, :, 0] + product[:, :, :, 1, :, 1]
    right_imag = product[:, :, :, 1, :, 0] - product[:, :, :, 0, :, 1]
    right = jnp.stack([right_real, right_imag], axis=3).astype(jnp.bfloat16)
    total = jnp.einsum("fnegpq,fnecqs->fnegcps", green, right, preferred_element_type=jnp.float32)
    out_real = total[:, :, :, 0, 0] - total[:, :, :, 1, 1]
    out_imag = total[:, :, :, 0, 1] + total[:, :, :, 1, 0]
    return jnp.stack([out_real, out_imag], axis=3)


def split_table(table):
    high_part = table.astype(jnp.bfloat16)
    low_part = (table - high_part.astype(jnp.float32)).astype(jnp.bfloat16)
    return (high_part, low_part)


def spectrum(values, table_high, table_low, padded_len):

    def apply_table(part):
        return jnp.dot(table_high, part, preferred_element_type=jnp.float32) + jnp.dot(
            table_low, part, preferred_element_type=jnp.float32
        )

    real_terms = apply_table(values[:, 0])
    imag_terms = apply_table(values[:, 1])
    out_real = real_terms[:padded_len] + imag_terms[padded_len:]
    out_imag = imag_terms[:padded_len] - real_terms[padded_len:]
    return (out_real, out_imag)


def body(green_lower, green_diag, green_upper, self_energy, coulomb):
    block_count = green_diag.shape[0]
    energy_local = green_diag.shape[1]
    block_order = green_diag.shape[-1]
    energies = energy_local * lax.axis_size("energy")
    padded_len = 2 * energies
    peers = lax.axis_size("space")
    on_chip = [(i, i ^ 1) for i in range(peers - peers % 2)]
    across = [(i, i + 1) for i in range(1, peers - 1, 2)]
    across = across + [(j, i) for i, j in across]
    neighbour = lax.ppermute(self_energy, "space", across)
    partner = lax.ppermute(self_energy, "space", on_chip)
    diag_term = congruence(green_diag, self_energy)
    even = lax.axis_index("space") % 2 == 0
    green_on = jnp.where(even, green_upper, green_lower)
    green_across = jnp.where(even, green_lower, green_upper)
    near_sum = diag_term + congruence(green_on, partner)
    near_sum, neighbour = lax.optimization_barrier((near_sum, neighbour))
    across_term = congruence(green_across, neighbour)
    total = near_sum + across_term
    groups = lax.axis_size("energy")
    total = total.reshape(2, block_count, energy_local, 2, groups, block_order // groups, block_order)
    outgoing = jnp.transpose(total, (4, 0, 2, 3, 1, 5, 6)).astype(jnp.bfloat16)
    outgoing = outgoing.reshape(groups, 2, energy_local, 2, -1)
    frequency = lax.iota(jnp.int32, padded_len)
    energy_index = lax.iota(jnp.int32, energies)
    step_angle = 2.0 * math.pi / padded_len
    forward_angle = (frequency[:, None] * energy_index[None, :] % padded_len).astype(
        jnp.float32
    ) * step_angle
    cos_table, sin_table = jnp.cos(forward_angle), jnp.sin(forward_angle)
    forward_table = jnp.concatenate(
        [
            jnp.stack([cos_table, sin_table], axis=-1),
            jnp.stack([-sin_table, cos_table], axis=-1),
        ],
        axis=0,
    ).astype(jnp.bfloat16)
    entries = lax.all_to_all(outgoing, "energy", 0, 0, tiled=True)
    spectra = jnp.einsum(
        "qxer,xfern->qfn",
        forward_table.reshape(2 * padded_len, groups, energy_local, 2),
        entries,
        preferred_element_type=jnp.float32,
    )
    spec_real = spectra[:padded_len]
    spec_imag = spectra[padded_len:]
    product_real = spec_real[:, 0] * spec_real[:, 1] + spec_imag[:, 0] * spec_imag[:, 1]
    product_imag = spec_imag[:, 0] * spec_real[:, 1] - spec_real[:, 0] * spec_imag[:, 1]
    stacked_product = jnp.concatenate([product_real, product_imag], axis=0)
    mirrored = (padded_len - energy_index) % padded_len

    def back_rows(lags):
        angle = (lags[:, None] * frequency[None, :] % padded_len).astype(jnp.float32) * step_angle
        cos_rows, sin_rows = jnp.cos(angle), jnp.sin(angle)
        real_rows = jnp.concatenate([cos_rows, -sin_rows], axis=1)
        imag_rows = jnp.concatenate([sin_rows, cos_rows], axis=1)
        return real_rows, imag_rows

    lesser_real, lesser_imag = back_rows(energy_index)
    greater_real, greater_imag = back_rows(mirrored)
    back_table = jnp.stack([lesser_real, lesser_imag, greater_real, -greater_imag], axis=1)
    back_table = back_table.reshape(4 * energies, 2 * padded_len)
    factor = 1.0 / (padded_len * math.sqrt(energies))
    combined = jnp.dot(
        back_table.astype(jnp.bfloat16),
        stacked_product.astype(jnp.bfloat16),
        preferred_element_type=jnp.float32,
    )
    polar = (combined * factor).astype(jnp.bfloat16).reshape(groups, energy_local, 2, 2, -1)
    returned = lax.all_to_all(polar, "energy", 0, 0, tiled=True)
    returned = returned.reshape(groups, energy_local, 2, 2, block_count, -1, block_order)
    coulomb_split = coulomb.reshape(block_count, block_order, groups, -1)
    left_product = jnp.einsum(
        "npxi,xeftnir->fetnpr", coulomb_split, returned, preferred_element_type=jnp.float32
    ).astype(jnp.bfloat16)
    screened = jnp.einsum(
        "fetnpr,nsr->fnetps", left_product, coulomb, preferred_element_type=jnp.float32
    )
    return screened.astype(jnp.bfloat16)


def solution(mesh):
    in_specs = (
        P("space", "energy", None, None, None),
        P("space", "energy", None, None, None),
        P("space", "energy", None, None, None),
        P(None, "space", "energy", None, None, None),
        P("space", None, None),
    )
    out_specs = P(None, "space", "energy", None, None, None)
    return jax.shard_map(body, mesh=mesh, in_specs=in_specs, out_specs=out_specs, check_vma=False)
```

```python
import math

import jax
import jax.numpy as jnp
from jax import lax
from jax.sharding import PartitionSpec as P


def padded_2(shard, sides, width):
    for axis, dim in sides:
        peers, length = (lax.axis_size(axis), shard.shape[dim])
        up = [(i, (i + 1) % peers) for i in range(peers - 1)]
        down = [(j, i) for i, j in up]
        last = lax.slice_in_dim(shard, length - width, length, axis=dim)
        initial = lax.slice_in_dim(shard, 0, width, axis=dim)
        before = lax.ppermute(last, axis, up)
        after = lax.ppermute(initial, axis, down)
        shard = jnp.concatenate([before, shard, after], axis=dim)
    return shard


def in_blocks(shard, dim, peers):
    before, after = (shard.shape[:dim], shard.shape[dim + 1 :])
    return jnp.moveaxis(shard.reshape(*before, peers, -1, *after), dim, 0)


def edges_of(length, count):
    unit = 8 if length >= 8 * count else 1
    return [length // unit * k // count * unit for k in range(1, count)]


def joined_along(tiles, dim):
    tiles = jnp.moveaxis(tiles, 0, dim)
    shape = tiles.shape
    return tiles.reshape(*shape[:dim], shape[dim] * shape[dim + 1], *shape[dim + 2 :])


def cut_exchange(shard, axis, pieces, split_dim, concat_dim):
    tiles = in_blocks(shard, split_dim, lax.axis_size(axis))
    split_at = max(range(1, max(2, tiles.ndim - 1)), key=lambda d: tiles.shape[d])
    gathered = []
    for slab in jnp.split(tiles, edges_of(tiles.shape[split_at], pieces), axis=split_at):
        if slab.size:
            gathered.append(lax.all_to_all(slab, axis, split_axis=0, concat_axis=0, tiled=True))
    return joined_along(jnp.concatenate(gathered, axis=split_at), concat_dim)


def congruence(green, sigma):
    green = jnp.broadcast_to(green[None], (sigma.shape[0],) + green.shape)
    product = jnp.einsum(
        "fneiqr,fnegsr->fneiqgs", sigma, green, preferred_element_type=jnp.float32
    )
    right_real = product[:, :, :, 0, :, 0] + product[:, :, :, 1, :, 1]
    right_imag = product[:, :, :, 1, :, 0] - product[:, :, :, 0, :, 1]
    right = jnp.stack([right_real, right_imag], axis=3).astype(jnp.bfloat16)
    total = jnp.einsum("fnegpq,fnecqs->fnegcps", green, right, preferred_element_type=jnp.float32)
    out_real = total[:, :, :, 0, 0] - total[:, :, :, 1, 1]
    out_imag = total[:, :, :, 0, 1] + total[:, :, :, 1, 0]
    return jnp.stack([out_real, out_imag], axis=3)


def split_table(table):
    high_part = table.astype(jnp.bfloat16)
    low_part = (table - high_part.astype(jnp.float32)).astype(jnp.bfloat16)
    return (high_part, low_part)


def spectrum(values, table_high, table_low, padded_len):

    def apply_table(part):
        return jnp.dot(table_high, part, preferred_element_type=jnp.float32) + jnp.dot(
            table_low, part, preferred_element_type=jnp.float32
        )

    real_terms = apply_table(values[:, 0])
    imag_terms = apply_table(values[:, 1])
    out_real = real_terms[:padded_len] + imag_terms[padded_len:]
    out_imag = imag_terms[:padded_len] - real_terms[padded_len:]
    return (out_real, out_imag)


def body(green_lower, green_diag, green_upper, self_energy, coulomb):
    block_count = green_diag.shape[0]
    energy_local = green_diag.shape[1]
    block_order = green_diag.shape[-1]
    energies = energy_local * lax.axis_size("energy")
    padded_len = 2 * energies
    peers = lax.axis_size("space")
    on_chip = [(i, i ^ 1) for i in range(peers - peers % 2)]
    across = [(i, i + 1) for i in range(1, peers - 1, 2)]
    across = across + [(j, i) for i, j in across]
    neighbour = lax.ppermute(self_energy, "space", across)
    partner = lax.ppermute(self_energy, "space", on_chip)
    diag_term = congruence(green_diag, self_energy)
    even = lax.axis_index("space") % 2 == 0
    green_on = jnp.where(even, green_upper, green_lower)
    green_across = jnp.where(even, green_lower, green_upper)
    near_sum = diag_term + congruence(green_on, partner)
    coulomb_split = jnp.transpose(
        coulomb.reshape(block_count, block_order, lax.axis_size("energy"), -1), (0, 2, 3, 1)
    )
    near_sum, neighbour, coulomb_split = lax.optimization_barrier((near_sum, neighbour, coulomb_split))
    across_term = congruence(green_across, neighbour)
    total = near_sum + across_term
    groups = lax.axis_size("energy")
    total = total.reshape(2, block_count, energy_local, 2, groups, block_order // groups, block_order)
    outgoing = jnp.transpose(total, (4, 0, 2, 3, 1, 5, 6)).astype(jnp.bfloat16)
    outgoing = outgoing.reshape(groups, 2, energy_local, 2, -1)
    frequency = lax.iota(jnp.int32, padded_len)
    energy_index = lax.iota(jnp.int32, energies)
    step_angle = 2.0 * math.pi / padded_len
    forward_angle = (frequency[:, None] * energy_index[None, :] % padded_len).astype(
        jnp.float32
    ) * step_angle
    cos_table, sin_table = jnp.cos(forward_angle), jnp.sin(forward_angle)
    forward_table = jnp.concatenate(
        [
            jnp.stack([cos_table, sin_table], axis=-1),
            jnp.stack([-sin_table, cos_table], axis=-1),
        ],
        axis=0,
    ).astype(jnp.bfloat16)
    entries = lax.all_to_all(outgoing, "energy", 0, 0, tiled=True)
    spectra = jnp.einsum(
        "qxer,xfern->qfn",
        forward_table.reshape(2 * padded_len, groups, energy_local, 2),
        entries,
        preferred_element_type=jnp.float32,
    )
    spec_real = spectra[:padded_len]
    spec_imag = spectra[padded_len:]
    product_real = spec_real[:, 0] * spec_real[:, 1] + spec_imag[:, 0] * spec_imag[:, 1]
    product_imag = spec_imag[:, 0] * spec_real[:, 1] - spec_real[:, 0] * spec_imag[:, 1]
    stacked_product = jnp.concatenate([product_real, product_imag], axis=0)
    mirrored = (padded_len - energy_index) % padded_len

    def back_rows(lags):
        angle = (lags[:, None] * frequency[None, :] % padded_len).astype(jnp.float32) * step_angle
        cos_rows, sin_rows = jnp.cos(angle), jnp.sin(angle)
        real_rows = jnp.concatenate([cos_rows, -sin_rows], axis=1)
        imag_rows = jnp.concatenate([sin_rows, cos_rows], axis=1)
        return real_rows, imag_rows

    lesser_real, lesser_imag = back_rows(energy_index)
    greater_real, greater_imag = back_rows(mirrored)
    back_table = jnp.stack([lesser_real, lesser_imag, greater_real, -greater_imag], axis=1)
    back_table = back_table.reshape(4 * energies, 2 * padded_len)
    factor = 1.0 / (padded_len * math.sqrt(energies))
    combined = jnp.dot(
        back_table.astype(jnp.bfloat16),
        stacked_product.astype(jnp.bfloat16),
        preferred_element_type=jnp.float32,
    )
    polar = (combined * factor).astype(jnp.bfloat16).reshape(groups, energy_local, 2, 2, -1)
    returned = lax.all_to_all(polar, "energy", 0, 0, tiled=True)
    returned = returned.reshape(groups, energy_local, 2, 2, block_count, -1, block_order)
    left_product = jnp.einsum(
        "nxip,xeftnir->fetnpr", coulomb_split, returned, preferred_element_type=jnp.float32
    ).astype(jnp.bfloat16)
    screened = jnp.einsum(
        "fetnpr,nsr->fnetps", left_product, coulomb, preferred_element_type=jnp.float32
    )
    return screened.astype(jnp.bfloat16)


def solution(mesh):
    in_specs = (
        P("space", "energy", None, None, None),
        P("space", "energy", None, None, None),
        P("space", "energy", None, None, None),
        P(None, "space", "energy", None, None, None),
        P("space", None, None),
    )
    out_specs = P(None, "space", "energy", None, None, None)
    return jax.shard_map(body, mesh=mesh, in_specs=in_specs, out_specs=out_specs, check_vma=False)
```

```python
import math

import jax
import jax.numpy as jnp
from jax import lax
from jax.sharding import PartitionSpec as P


def padded_2(shard, sides, width):
    for axis, dim in sides:
        peers, length = (lax.axis_size(axis), shard.shape[dim])
        up = [(i, (i + 1) % peers) for i in range(peers - 1)]
        down = [(j, i) for i, j in up]
        last = lax.slice_in_dim(shard, length - width, length, axis=dim)
        initial = lax.slice_in_dim(shard, 0, width, axis=dim)
        before = lax.ppermute(last, axis, up)
        after = lax.ppermute(initial, axis, down)
        shard = jnp.concatenate([before, shard, after], axis=dim)
    return shard


def in_blocks(shard, dim, peers):
    before, after = (shard.shape[:dim], shard.shape[dim + 1 :])
    return jnp.moveaxis(shard.reshape(*before, peers, -1, *after), dim, 0)


def edges_of(length, count):
    unit = 8 if length >= 8 * count else 1
    return [length // unit * k // count * unit for k in range(1, count)]


def joined_along(tiles, dim):
    tiles = jnp.moveaxis(tiles, 0, dim)
    shape = tiles.shape
    return tiles.reshape(*shape[:dim], shape[dim] * shape[dim + 1], *shape[dim + 2 :])


def cut_exchange(shard, axis, pieces, split_dim, concat_dim):
    tiles = in_blocks(shard, split_dim, lax.axis_size(axis))
    split_at = max(range(1, max(2, tiles.ndim - 1)), key=lambda d: tiles.shape[d])
    gathered = []
    for slab in jnp.split(tiles, edges_of(tiles.shape[split_at], pieces), axis=split_at):
        if slab.size:
            gathered.append(lax.all_to_all(slab, axis, split_axis=0, concat_axis=0, tiled=True))
    return joined_along(jnp.concatenate(gathered, axis=split_at), concat_dim)


def congruence(green, sigma):
    green = jnp.broadcast_to(green[None], (sigma.shape[0],) + green.shape)
    product = jnp.einsum(
        "fneiqr,fnegsr->fneiqgs", sigma, green, preferred_element_type=jnp.float32
    )
    right_real = product[:, :, :, 0, :, 0] + product[:, :, :, 1, :, 1]
    right_imag = product[:, :, :, 1, :, 0] - product[:, :, :, 0, :, 1]
    right = jnp.stack([right_real, right_imag], axis=3).astype(jnp.bfloat16)
    total = jnp.einsum("fnegpq,fnecqs->fnegcps", green, right, preferred_element_type=jnp.float32)
    out_real = total[:, :, :, 0, 0] - total[:, :, :, 1, 1]
    out_imag = total[:, :, :, 0, 1] + total[:, :, :, 1, 0]
    return jnp.stack([out_real, out_imag], axis=3)


def split_table(table):
    high_part = table.astype(jnp.bfloat16)
    low_part = (table - high_part.astype(jnp.float32)).astype(jnp.bfloat16)
    return (high_part, low_part)


def spectrum(values, table_high, table_low, padded_len):

    def apply_table(part):
        return jnp.dot(table_high, part, preferred_element_type=jnp.float32) + jnp.dot(
            table_low, part, preferred_element_type=jnp.float32
        )

    real_terms = apply_table(values[:, 0])
    imag_terms = apply_table(values[:, 1])
    out_real = real_terms[:padded_len] + imag_terms[padded_len:]
    out_imag = imag_terms[:padded_len] - real_terms[padded_len:]
    return (out_real, out_imag)


def body(green_lower, green_diag, green_upper, self_energy, coulomb):
    block_count = green_diag.shape[0]
    energy_local = green_diag.shape[1]
    block_order = green_diag.shape[-1]
    energies = energy_local * lax.axis_size("energy")
    padded_len = 2 * energies
    peers = lax.axis_size("space")
    on_chip = [(i, i ^ 1) for i in range(peers - peers % 2)]
    across = [(i, i + 1) for i in range(1, peers - 1, 2)]
    across = across + [(j, i) for i, j in across]
    neighbour = lax.ppermute(self_energy, "space", across)
    partner = lax.ppermute(self_energy, "space", on_chip)
    diag_term = congruence(green_diag, self_energy)
    even = lax.axis_index("space") % 2 == 0
    green_on = jnp.where(even, green_upper, green_lower)
    green_across = jnp.where(even, green_lower, green_upper)
    near_sum = diag_term + congruence(green_on, partner)
    near_sum, neighbour = lax.optimization_barrier((near_sum, neighbour))
    across_term = congruence(green_across, neighbour)
    total = near_sum + across_term
    groups = lax.axis_size("energy")
    total = total.reshape(2, block_count, energy_local, 2, groups, block_order // groups, block_order)
    outgoing = jnp.transpose(total, (4, 0, 2, 3, 1, 5, 6)).astype(jnp.bfloat16)
    outgoing = outgoing.reshape(groups, 2, energy_local, 2, -1)
    frequency = lax.iota(jnp.int32, padded_len)
    energy_index = lax.iota(jnp.int32, energies)
    step_angle = 2.0 * math.pi / padded_len
    forward_angle = (frequency[:, None] * energy_index[None, :] % padded_len).astype(
        jnp.float32
    ) * step_angle
    cos_table, sin_table = jnp.cos(forward_angle), jnp.sin(forward_angle)
    forward_table = jnp.concatenate(
        [
            jnp.stack([cos_table, sin_table], axis=-1),
            jnp.stack([-sin_table, cos_table], axis=-1),
        ],
        axis=0,
    ).astype(jnp.bfloat16)
    entries = lax.all_to_all(outgoing, "energy", 0, 0, tiled=True)
    spectra = jnp.einsum(
        "qxer,xfern->qfn",
        forward_table.reshape(2 * padded_len, groups, energy_local, 2),
        entries,
        preferred_element_type=jnp.float32,
    )
    spec_real = spectra[:padded_len]
    spec_imag = spectra[padded_len:]
    product_real = spec_real[:, 0] * spec_real[:, 1] + spec_imag[:, 0] * spec_imag[:, 1]
    product_imag = spec_imag[:, 0] * spec_real[:, 1] - spec_real[:, 0] * spec_imag[:, 1]
    stacked_product = jnp.concatenate([product_real, product_imag], axis=0)
    mirrored = (padded_len - energy_index) % padded_len

    def back_rows(lags):
        angle = (lags[:, None] * frequency[None, :] % padded_len).astype(jnp.float32) * step_angle
        cos_rows, sin_rows = jnp.cos(angle), jnp.sin(angle)
        real_rows = jnp.concatenate([cos_rows, -sin_rows], axis=1)
        imag_rows = jnp.concatenate([sin_rows, cos_rows], axis=1)
        return real_rows, imag_rows

    lesser_real, lesser_imag = back_rows(energy_index)
    greater_real, greater_imag = back_rows(mirrored)
    back_table = jnp.stack([lesser_real, lesser_imag, greater_real, -greater_imag], axis=1)
    back_table = back_table.reshape(4 * energies, 2 * padded_len)
    factor = 1.0 / (padded_len * math.sqrt(energies))
    combined = jnp.dot(
        back_table.astype(jnp.bfloat16),
        stacked_product.astype(jnp.bfloat16),
        preferred_element_type=jnp.float32,
    )
    polar = (combined * factor).astype(jnp.bfloat16).reshape(groups, energy_local, 2, 2, -1)
    polar = polar.reshape(groups, 4 * energy_local, -1)
    returned = lax.all_to_all(polar, "energy", 0, 0, tiled=True)
    returned = returned.reshape(groups, energy_local, 2, 2, block_count, -1, block_order)
    returned = jnp.transpose(returned, (2, 1, 3, 4, 0, 5, 6))
    returned = returned.reshape(2, energy_local, 2, block_count, block_order, block_order)
    left_product = jnp.einsum(
        "npq,fetnqr->fetnpr", coulomb, returned, preferred_element_type=jnp.float32
    ).astype(jnp.bfloat16)
    screened = jnp.einsum(
        "fetnpr,nsr->fnetps", left_product, coulomb, preferred_element_type=jnp.float32
    )
    return screened.astype(jnp.bfloat16)


def solution(mesh):
    in_specs = (
        P("space", "energy", None, None, None),
        P("space", "energy", None, None, None),
        P("space", "energy", None, None, None),
        P(None, "space", "energy", None, None, None),
        P("space", None, None),
    )
    out_specs = P(None, "space", "energy", None, None, None)
    return jax.shard_map(body, mesh=mesh, in_specs=in_specs, out_specs=out_specs, check_vma=False)
```

```python
import math

import jax
import jax.numpy as jnp
from jax import lax
from jax.sharding import PartitionSpec as P


def padded_2(shard, sides, width):
    for axis, dim in sides:
        peers, length = (lax.axis_size(axis), shard.shape[dim])
        up = [(i, (i + 1) % peers) for i in range(peers - 1)]
        down = [(j, i) for i, j in up]
        last = lax.slice_in_dim(shard, length - width, length, axis=dim)
        initial = lax.slice_in_dim(shard, 0, width, axis=dim)
        before = lax.ppermute(last, axis, up)
        after = lax.ppermute(initial, axis, down)
        shard = jnp.concatenate([before, shard, after], axis=dim)
    return shard


def in_blocks(shard, dim, peers):
    before, after = (shard.shape[:dim], shard.shape[dim + 1 :])
    return jnp.moveaxis(shard.reshape(*before, peers, -1, *after), dim, 0)


def edges_of(length, count):
    unit = 8 if length >= 8 * count else 1
    return [length // unit * k // count * unit for k in range(1, count)]


def joined_along(tiles, dim):
    tiles = jnp.moveaxis(tiles, 0, dim)
    shape = tiles.shape
    return tiles.reshape(*shape[:dim], shape[dim] * shape[dim + 1], *shape[dim + 2 :])


def cut_exchange(shard, axis, pieces, split_dim, concat_dim):
    tiles = in_blocks(shard, split_dim, lax.axis_size(axis))
    split_at = max(range(1, max(2, tiles.ndim - 1)), key=lambda d: tiles.shape[d])
    gathered = []
    for slab in jnp.split(tiles, edges_of(tiles.shape[split_at], pieces), axis=split_at):
        if slab.size:
            gathered.append(lax.all_to_all(slab, axis, split_axis=0, concat_axis=0, tiled=True))
    return joined_along(jnp.concatenate(gathered, axis=split_at), concat_dim)


def congruence(green, sigma):
    green = jnp.broadcast_to(green[None], (sigma.shape[0],) + green.shape)
    product = jnp.einsum(
        "fneiqr,fnegsr->fneiqgs", sigma, green, preferred_element_type=jnp.float32
    )
    right_real = product[:, :, :, 0, :, 0] + product[:, :, :, 1, :, 1]
    right_imag = product[:, :, :, 1, :, 0] - product[:, :, :, 0, :, 1]
    right = jnp.stack([right_real, right_imag], axis=3).astype(jnp.bfloat16)
    total = jnp.einsum("fnegpq,fnecqs->fnegcps", green, right, preferred_element_type=jnp.float32)
    out_real = total[:, :, :, 0, 0] - total[:, :, :, 1, 1]
    out_imag = total[:, :, :, 0, 1] + total[:, :, :, 1, 0]
    return jnp.stack([out_real, out_imag], axis=3)


def split_table(table):
    high_part = table.astype(jnp.bfloat16)
    low_part = (table - high_part.astype(jnp.float32)).astype(jnp.bfloat16)
    return (high_part, low_part)


def spectrum(values, table_high, table_low, padded_len):

    def apply_table(part):
        return jnp.dot(table_high, part, preferred_element_type=jnp.float32) + jnp.dot(
            table_low, part, preferred_element_type=jnp.float32
        )

    real_terms = apply_table(values[:, 0])
    imag_terms = apply_table(values[:, 1])
    out_real = real_terms[:padded_len] + imag_terms[padded_len:]
    out_imag = imag_terms[:padded_len] - real_terms[padded_len:]
    return (out_real, out_imag)


def body(green_lower, green_diag, green_upper, self_energy, coulomb):
    block_count = green_diag.shape[0]
    energy_local = green_diag.shape[1]
    block_order = green_diag.shape[-1]
    energies = energy_local * lax.axis_size("energy")
    padded_len = 2 * energies
    peers = lax.axis_size("space")
    on_chip = [(i, i ^ 1) for i in range(peers - peers % 2)]
    across = [(i, i + 1) for i in range(1, peers - 1, 2)]
    across = across + [(j, i) for i, j in across]
    neighbour = lax.ppermute(self_energy, "space", across)
    partner = lax.ppermute(self_energy, "space", on_chip)
    diag_term = congruence(green_diag, self_energy)
    even = lax.axis_index("space") % 2 == 0
    green_on = jnp.where(even, green_upper, green_lower)
    green_across = jnp.where(even, green_lower, green_upper)
    near_sum = diag_term + congruence(green_on, partner)
    coulomb_split = jnp.transpose(
        coulomb.reshape(block_count, block_order, lax.axis_size("energy"), -1), (0, 2, 3, 1)
    )
    near_sum, neighbour, coulomb_split = lax.optimization_barrier((near_sum, neighbour, coulomb_split))
    across_term = congruence(green_across, neighbour)
    total = near_sum + across_term
    groups = lax.axis_size("energy")
    total = total.reshape(2, block_count, energy_local, 2, groups, block_order // groups, block_order)
    outgoing = jnp.transpose(total, (4, 0, 2, 3, 1, 5, 6)).astype(jnp.bfloat16)
    outgoing = outgoing.reshape(groups, 2, energy_local, 2, -1)
    frequency = lax.iota(jnp.int32, padded_len)
    energy_index = lax.iota(jnp.int32, energies)
    step_angle = 2.0 * math.pi / padded_len
    forward_angle = (frequency[:, None] * energy_index[None, :] % padded_len).astype(
        jnp.float32
    ) * step_angle
    cos_table, sin_table = jnp.cos(forward_angle), jnp.sin(forward_angle)
    forward_table = jnp.concatenate(
        [
            jnp.stack([cos_table, sin_table], axis=-1),
            jnp.stack([-sin_table, cos_table], axis=-1),
        ],
        axis=0,
    ).astype(jnp.bfloat16)
    entries = lax.all_to_all(outgoing, "energy", 0, 0, tiled=True)
    spectra = jnp.einsum(
        "qxer,xfern->qfn",
        forward_table.reshape(2 * padded_len, groups, energy_local, 2),
        entries,
        preferred_element_type=jnp.float32,
    )
    spec_real = spectra[:padded_len]
    spec_imag = spectra[padded_len:]
    product_real = spec_real[:, 0] * spec_real[:, 1] + spec_imag[:, 0] * spec_imag[:, 1]
    product_imag = spec_imag[:, 0] * spec_real[:, 1] - spec_real[:, 0] * spec_imag[:, 1]
    stacked_product = jnp.concatenate([product_real, product_imag], axis=0)
    mirrored = (padded_len - energy_index) % padded_len

    def back_rows(lags):
        angle = (lags[:, None] * frequency[None, :] % padded_len).astype(jnp.float32) * step_angle
        cos_rows, sin_rows = jnp.cos(angle), jnp.sin(angle)
        real_rows = jnp.concatenate([cos_rows, -sin_rows], axis=1)
        imag_rows = jnp.concatenate([sin_rows, cos_rows], axis=1)
        return real_rows, imag_rows

    lesser_real, lesser_imag = back_rows(energy_index)
    greater_real, greater_imag = back_rows(mirrored)
    back_table = jnp.stack([lesser_real, lesser_imag, greater_real, -greater_imag], axis=1)
    back_table = back_table.reshape(4 * energies, 2 * padded_len)
    factor = 1.0 / (padded_len * math.sqrt(energies))
    combined = jnp.dot(
        back_table.astype(jnp.bfloat16),
        stacked_product.astype(jnp.bfloat16),
        preferred_element_type=jnp.float32,
    )
    polar = (combined * factor).astype(jnp.bfloat16).reshape(groups, energy_local, 2, 2, -1)
    polar = polar.reshape(groups, 4 * energy_local, -1)
    returned = lax.all_to_all(polar, "energy", 0, 0, tiled=True)
    returned = returned.reshape(groups, energy_local, 2, 2, block_count, -1, block_order)
    left_product = jnp.einsum(
        "nxip,xeftnir->fetnpr", coulomb_split, returned, preferred_element_type=jnp.float32
    ).astype(jnp.bfloat16)
    screened = jnp.einsum(
        "fetnpr,nsr->fnetps", left_product, coulomb, preferred_element_type=jnp.float32
    )
    return screened.astype(jnp.bfloat16)


def solution(mesh):
    in_specs = (
        P("space", "energy", None, None, None),
        P("space", "energy", None, None, None),
        P("space", "energy", None, None, None),
        P(None, "space", "energy", None, None, None),
        P("space", None, None),
    )
    out_specs = P(None, "space", "energy", None, None, None)
    return jax.shard_map(body, mesh=mesh, in_specs=in_specs, out_specs=out_specs, check_vma=False)
```
